512 devices in a mesh: smp: 16 (over z), par: 32 (over x, y, core).
Axes of the slice: x: 4, y: 4, z: 16, core: 2. Of those that a mesh axis runs over, the one named last changes fastest.
Arguments:
- jacobian: bfloat16 [4096, 16384], P('smp', 'par'), may hold values from -52 to 52
Outputs:
- panel_factor: float32 [4096, 512], P('smp')
- schur_part: float32 [4096, 4096], P('smp', 'par')
The draws below stay inside these ranges and needn't reach their ends.
All inputs are finite; a program needn't handle non-finite values.
Results may differ from the reference program's by a relative error of at most 0.0022.
Values may be sent and summed in bfloat16 or wider, within the bound.
No kernel may reach another device: no remote copies, remote signals or barrier semaphores. Data moves between devices by JAX's collectives and lax.ppermute only.
A program may use at most 64 MiB of HBM per device.

```python
import math
import jax
import jax.numpy as jnp
from jax import lax

PANEL = 512
SAMPLES = 4096
PARAMS = 16384


def draw_jacobian(key, part):
    keys = jax.random.split(jax.random.fold_in(key, 17), 5)
    ramp = jnp.arange(SAMPLES, dtype=jnp.float32)[:, None] / (SAMPLES - 1)
    col_mean = jnp.clip(2.0 * jax.random.normal(keys[0], (1, PARAMS), jnp.float32), -6.0, 6.0)
    noise = jnp.clip(jax.random.normal(keys[4], (SAMPLES, PARAMS), jnp.float32), -5.0, 5.0)
    jitter = jax.random.uniform(keys[1], (SAMPLES, 1), jnp.float32, 0.0, math.log(1.28))
    row_scale = jnp.exp(ramp * math.log(2.5) + jitter)
    coeffs = jnp.clip(jax.random.normal(keys[2], (SAMPLES, 1), jnp.float32), -3.0, 3.0)
    common = jnp.clip(jax.random.normal(keys[3], (1, PARAMS), jnp.float32), -3.0, 3.0)
    values = col_mean + row_scale * (noise + coeffs * common)
    return values.astype(jnp.bfloat16)


def setup_inputs(seed: int = 0) -> dict:
    arg_keys = jax.random.split(jax.random.key(seed), 2)
    jacobian = draw_jacobian(jax.random.fold_in(arg_keys[1], 71), 0)
    return {"jacobian": jacobian}


shift_scale = 0.01

def reference(jacobian):
    widened = jacobian.astype(jnp.float32)
    col_mean = jnp.sum(widened, axis=0) / SAMPLES
    centered = (widened - col_mean).astype(jnp.bfloat16)
    centered = lax.optimization_barrier(centered).astype(jnp.float32)
    gram = jnp.dot(centered, centered.T, precision=lax.Precision.HIGHEST) / PARAMS
    trace_total = jnp.sum(jnp.diagonal(gram))
    shifted = gram + shift_scale * trace_total / SAMPLES * jnp.eye(SAMPLES, dtype=jnp.float32)
    factor = jnp.linalg.cholesky(shifted[:PANEL, :PANEL])
    panel_factor = jax.scipy.linalg.solve_triangular(factor, shifted[:, :PANEL].T, lower=True).T
    schur_part = shifted - jnp.dot(panel_factor, panel_factor.T, precision=lax.Precision.HIGHEST)
    return (panel_factor, schur_part)
```

```python
import jax
import jax.numpy as jnp
from jax import lax
from jax.sharding import PartitionSpec as P

PANEL = 512


shift_scale = 0.01


def shards(jacobian):
    row_count, par_width = jacobian.shape
    par_count = lax.axis_size("par")
    smp_count = lax.axis_size("smp")
    sample_total = row_count * smp_count
    param_total = par_width * par_count
    col_width = sample_total // par_count
    panel_piece = PANEL // par_count
    band_piece = col_width // smp_count
    row_index = lax.axis_index("smp")
    col_index = lax.axis_index("par")
    f32 = jnp.float32

    gathered = lax.all_gather(jacobian, "smp", axis=0, tiled=True)
    widened = gathered.astype(f32)
    col_mean = jnp.sum(widened, axis=0) / sample_total
    centered = (widened - col_mean).astype(jnp.bfloat16)
    mine = lax.dynamic_slice_in_dim(centered, row_index * row_count, row_count, 0)
    head = centered[:PANEL]
    contract = (((1,), (1,)), ((), ()))

    main = lax.dot_general(centered, mine, contract, preferred_element_type=f32)
    square = lax.dot_general(head, head, contract, preferred_element_type=f32)
    band_rows = lax.dynamic_index_in_dim(
        centered.reshape(par_count, smp_count, band_piece, par_width), row_index, 1, False
    ).reshape(par_count * band_piece, par_width)
    band = lax.dot_general(band_rows, head, contract, preferred_element_type=f32)
    sq = centered.astype(f32)
    sumsq = jnp.sum(sq * sq)

    width = row_count
    pieces = [
        main.reshape(par_count, col_width, width),
        main[:PANEL].reshape(par_count, panel_piece, width),
        square.reshape(par_count, panel_piece * PANEL // width, width),
        jnp.broadcast_to(sumsq, (par_count, 8, width)),
        band.reshape(par_count, band_piece * PANEL // width, width),
    ]
    stacked = jnp.concatenate(pieces, axis=1)
    chunk = stacked.shape[1]
    reduced = lax.psum_scatter(
        stacked.reshape(par_count * chunk, width), "par", scatter_dimension=0, tiled=True
    ) / param_total

    o1 = col_width
    o2 = o1 + panel_piece
    o3 = o2 + panel_piece * PANEL // width
    o4 = o3 + 8
    tile = reduced[:o1].T
    shared = lax.all_gather(reduced[o1:o4], "par", axis=0, tiled=False)
    band_mine = lax.all_gather(
        reduced[o4:].reshape(band_piece, PANEL), "smp", axis=0, tiled=True
    )
    panel_t = shared[:, : o2 - o1].reshape(PANEL, width)
    square_g = shared[:, o2 - o1 : o3 - o1].reshape(PANEL, PANEL)
    trace_total = shared[0, o3 - o1, 0]
    shift_value = shift_scale * trace_total / sample_total

    eye = jnp.arange(PANEL, dtype=jnp.int32)
    global_rows = row_index * row_count + jnp.arange(row_count, dtype=jnp.int32)
    global_cols = col_index * col_width + jnp.arange(col_width, dtype=jnp.int32)
    square_s = square_g + jnp.where(eye[:, None] == eye[None, :], shift_value, 0.0)
    panel_s = panel_t.T + jnp.where(global_rows[:, None] == eye[None, :], shift_value, 0.0)
    band_s = band_mine + jnp.where(global_cols[:, None] == eye[None, :], shift_value, 0.0)
    tile_s = tile + jnp.where(global_rows[:, None] == global_cols[None, :], shift_value, 0.0)

    factor = jnp.linalg.cholesky(square_s)
    panel_out = jax.scipy.linalg.solve_triangular(factor, panel_s.T, lower=True).T
    band_factor = jax.scipy.linalg.solve_triangular(factor, band_s.T, lower=True)
    schur_tile = tile_s - jnp.dot(panel_out, band_factor, precision=lax.Precision.HIGHEST)
    return (panel_out, schur_tile)


def solution(mesh):
    placed = (P("smp", "par"),)
    return jax.shard_map(
        shards,
        mesh=mesh,
        in_specs=placed,
        out_specs=(P("smp", None), P("smp", "par")),
        check_vma=False,
    )
```

```python
import jax
import jax.numpy as jnp
from jax import lax
from jax.sharding import PartitionSpec as P

PANEL = 512


shift_scale = 0.01


def shards(jacobian):
    row_count, par_width = jacobian.shape
    par_count = lax.axis_size("par")
    smp_count = lax.axis_size("smp")
    sample_total = row_count * smp_count
    param_total = par_width * par_count
    col_width = sample_total // par_count
    panel_piece = PANEL // par_count
    row_index = lax.axis_index("smp")
    col_index = lax.axis_index("par")
    f32 = jnp.float32

    gathered = lax.all_gather(jacobian, "smp", axis=0, tiled=True)
    widened = gathered.astype(f32)
    col_mean = jnp.sum(widened, axis=0) / sample_total
    centered = (widened - col_mean).astype(jnp.bfloat16)
    mine = lax.dynamic_slice_in_dim(centered, row_index * row_count, row_count, 0)
    head = centered[:PANEL]
    contract = (((1,), (1,)), ((), ()))

    main = lax.dot_general(centered, mine, contract, preferred_element_type=f32)
    square = lax.dot_general(head, head, contract, preferred_element_type=f32)
    band = lax.dot_general(centered, head, contract, preferred_element_type=f32)
    sq = centered.astype(f32)
    sumsq = jnp.sum(sq * sq)

    width = row_count
    panel_parts = jnp.concatenate(
        [
            main[:PANEL].reshape(par_count, panel_piece, width),
            square.reshape(par_count, panel_piece * PANEL // width, width),
            jnp.broadcast_to(sumsq, (par_count, 8, width)),
        ],
        axis=1,
    )
    chunk = panel_parts.shape[1]
    reduced = lax.psum_scatter(
        panel_parts.reshape(par_count * chunk, width), "par", scatter_dimension=0, tiled=True
    ) / param_total
    shared = lax.all_gather(reduced, "par", axis=0, tiled=False)

    main_parts = jnp.concatenate(
        [
            main.reshape(par_count, col_width, width),
            band.reshape(par_count, col_width * PANEL // width, width),
        ],
        axis=1,
    )
    main_parts, shared = lax.optimization_barrier((main_parts, shared))
    main_chunk = main_parts.shape[1]
    reduced_main = lax.psum_scatter(
        main_parts.reshape(par_count * main_chunk, width), "par", scatter_dimension=0, tiled=True
    ) / param_total
    tile = reduced_main[:col_width].T
    band_mine = reduced_main[col_width:].reshape(col_width, PANEL)

    o2 = panel_piece
    o3 = o2 + panel_piece * PANEL // width
    panel_t = shared[:, :o2].reshape(PANEL, width)
    square_g = shared[:, o2:o3].reshape(PANEL, PANEL)
    trace_total = shared[0, o3, 0]
    shift_value = shift_scale * trace_total / sample_total

    eye = jnp.arange(PANEL, dtype=jnp.int32)
    global_rows = row_index * row_count + jnp.arange(row_count, dtype=jnp.int32)
    global_cols = col_index * col_width + jnp.arange(col_width, dtype=jnp.int32)
    square_s = square_g + jnp.where(eye[:, None] == eye[None, :], shift_value, 0.0)
    panel_s = panel_t.T + jnp.where(global_rows[:, None] == eye[None, :], shift_value, 0.0)
    band_s = band_mine + jnp.where(global_cols[:, None] == eye[None, :], shift_value, 0.0)
    tile_s = tile + jnp.where(global_rows[:, None] == global_cols[None, :], shift_value, 0.0)

    factor = jnp.linalg.cholesky(square_s)
    panel_out = jax.scipy.linalg.solve_triangular(factor, panel_s.T, lower=True).T
    band_factor = jax.scipy.linalg.solve_triangular(factor, band_s.T, lower=True)
    schur_tile = tile_s - jnp.dot(panel_out, band_factor, precision=lax.Precision.HIGHEST)
    return (panel_out, schur_tile)


def solution(mesh):
    placed = (P("smp", "par"),)
    return jax.shard_map(
        shards,
        mesh=mesh,
        in_specs=placed,
        out_specs=(P("smp", None), P("smp", "par")),
        check_vma=False,
    )
```

```python
import jax
import jax.numpy as jnp
from jax import lax
from jax.sharding import Mesh, PartitionSpec as P

PANEL = 512


shift_scale = 0.01

PAR_PARTS = ("px", "py", "pc")


def reduce_in_steps(x, axes):
    for n, axis in enumerate(axes):
        if n:
            x = lax.optimization_barrier(x)
        x = lax.psum(x, axis)
    return x


def shards(jacobian):
    row_count, par_width = jacobian.shape
    sizes = [lax.axis_size(a) for a in PAR_PARTS]
    par_count = sizes[0] * sizes[1] * sizes[2]
    smp_count = lax.axis_size("smp")
    sample_total = row_count * smp_count
    param_total = par_width * par_count
    col_width = sample_total // par_count
    row_index = lax.axis_index("smp")
    col_index = (
        lax.axis_index("px") * (sizes[1] * sizes[2]) + lax.axis_index("py") * sizes[2] + lax.axis_index("pc")
    )
    f32 = jnp.float32

    gathered = lax.all_gather(jacobian, "smp", axis=0, tiled=True)
    widened = gathered.astype(f32)
    col_mean = jnp.sum(widened, axis=0) / sample_total
    centered = (widened - col_mean).astype(jnp.bfloat16)
    mine = lax.dynamic_slice_in_dim(centered, row_index * row_count, row_count, 0)
    head = centered[:PANEL]
    lhs = jnp.concatenate([mine, head], axis=0)
    contract = (((1,), (1,)), ((), ()))

    sq = centered.astype(f32)
    sumsq = jnp.sum(sq * sq)
    panel_all = lax.dot_general(lhs, head, contract, preferred_element_type=f32)
    panel_in = jnp.concatenate([panel_all, jnp.broadcast_to(sumsq, (8, PANEL))], axis=0)
    panel_red = reduce_in_steps(panel_in, ("pc", "py", "px")) / param_total

    big = lax.dot_general(lhs, centered, contract, preferred_element_type=f32)
    big, panel_red = lax.optimization_barrier((big, panel_red))
    big = lax.psum_scatter(big, PAR_PARTS, scatter_dimension=1, tiled=True)
    big = big / param_total
    tile = big[:row_count]
    band_t = big[row_count:]

    panel_g = panel_red[:row_count]
    square_g = panel_red[row_count : row_count + PANEL]
    trace_total = panel_red[row_count + PANEL, 0]
    shift_value = shift_scale * trace_total / sample_total

    eye = jnp.arange(PANEL, dtype=jnp.int32)
    global_rows = row_index * row_count + jnp.arange(row_count, dtype=jnp.int32)
    global_cols = col_index * col_width + jnp.arange(col_width, dtype=jnp.int32)
    square_s = square_g + jnp.where(eye[:, None] == eye[None, :], shift_value, 0.0)
    panel_s = panel_g + jnp.where(global_rows[:, None] == eye[None, :], shift_value, 0.0)
    band_s = band_t + jnp.where(eye[:, None] == global_cols[None, :], shift_value, 0.0)
    tile_s = tile + jnp.where(global_rows[:, None] == global_cols[None, :], shift_value, 0.0)

    factor = jnp.linalg.cholesky(square_s)
    panel_out = jax.scipy.linalg.solve_triangular(factor, panel_s.T, lower=True).T
    band_factor = jax.scipy.linalg.solve_triangular(factor, band_s, lower=True)
    schur_tile = tile_s - jnp.dot(panel_out, band_factor, precision=lax.Precision.HIGHEST)
    return (panel_out, schur_tile)


def solution(mesh):
    smp_count = mesh.shape["smp"]
    split = Mesh(mesh.devices.reshape(smp_count, 4, 4, -1), ("smp",) + PAR_PARTS)
    return jax.shard_map(
        shards,
        mesh=split,
        in_specs=(P("smp", PAR_PARTS),),
        out_specs=(P("smp", None), P("smp", PAR_PARTS)),
        check_vma=False,
    )
```

```python
import functools

import jax
import jax.numpy as jnp
from jax import lax
from jax.experimental import pallas as pl
from jax.experimental.pallas import tpu as pltpu
from jax.sharding import PartitionSpec as P

PANEL = 512


shift_scale = 0.01


HI = lax.Precision.HIGHEST
NT = (((1,), (1,)), ((), ()))


def _chol_kernel(a_ref, l_ref, w_ref, s_ref, blk_a, blk_b, blk_lt, blk_w, *, n, b):
    nb = n // b
    f32 = jnp.float32
    s_ref[...] = a_ref[...]
    l_ref[...] = jnp.zeros((n, n), f32)
    w_ref[...] = jnp.zeros((n, n), f32)
    rows = lax.broadcasted_iota(jnp.int32, (b, b), 0)
    cols = lax.broadcasted_iota(jnp.int32, (b, b), 1)
    lane = lax.broadcasted_iota(jnp.int32, (1, b), 1)
    for k in range(nb):
        ks = pl.ds(k * b, b)
        blk_a[...] = s_ref[ks, ks]
        blk_b[...] = jnp.where(rows == cols, 1.0, 0.0).astype(f32)

        def step(j, carry):
            row = blk_a[pl.ds(j, 1), :]
            d = jnp.sum(jnp.where(lane == j, row, 0.0), axis=1, keepdims=True)
            s = jnp.sqrt(d)
            v_row = jnp.where(lane >= j, row / s, 0.0)
            v_col = jnp.transpose(jnp.broadcast_to(v_row, (8, b)))[:, 0:1]
            blk_a[...] = blk_a[...] - v_col * v_row
            x = blk_b[pl.ds(j, 1), :] / s
            blk_b[...] = blk_b[...] - v_col * x
            blk_lt[pl.ds(j, 1), :] = v_row
            blk_w[pl.ds(j, 1), :] = x
            return carry

        lax.fori_loop(0, b, step, 0)
        w_kk = blk_w[...]
        l_ref[ks, ks] = jnp.transpose(blk_lt[...])
        w_ref[ks, ks] = w_kk
        if k < nb - 1:
            rest = pl.ds((k + 1) * b, n - (k + 1) * b)
            below = lax.dot_general(s_ref[rest, ks], w_kk, NT, precision=HI, preferred_element_type=f32)
            l_ref[rest, ks] = below
            s_ref[rest, rest] = s_ref[rest, rest] - lax.dot_general(
                below, below, NT, precision=HI, preferred_element_type=f32
            )
    for i in range(1, nb):
        w_ii = w_ref[pl.ds(i * b, b), pl.ds(i * b, b)]
        for j in range(i):
            acc = jnp.zeros((b, b), f32)
            for m in range(j, i):
                acc = acc + jnp.dot(
                    l_ref[pl.ds(i * b, b), pl.ds(m * b, b)],
                    w_ref[pl.ds(m * b, b), pl.ds(j * b, b)],
                    precision=HI,
                    preferred_element_type=f32,
                )
            w_ref[pl.ds(i * b, b), pl.ds(j * b, b)] = -jnp.dot(
                w_ii, acc, precision=HI, preferred_element_type=f32
            )


def chol_and_inverse(a, block=128):
    n = a.shape[0]
    f32 = jnp.float32
    return pl.pallas_call(
        functools.partial(_chol_kernel, n=n, b=block),
        out_shape=(jax.ShapeDtypeStruct((n, n), f32), jax.ShapeDtypeStruct((n, n), f32)),
        in_specs=[pl.BlockSpec(memory_space=pltpu.VMEM)],
        out_specs=(pl.BlockSpec(memory_space=pltpu.VMEM), pl.BlockSpec(memory_space=pltpu.VMEM)),
        scratch_shapes=[
            pltpu.VMEM((n, n), f32),
            pltpu.VMEM((block, block), f32),
            pltpu.VMEM((block, block), f32),
            pltpu.VMEM((block, block), f32),
            pltpu.VMEM((block, block), f32),
        ],
        cost_estimate=pl.CostEstimate(flops=2 * n * n * n, bytes_accessed=3 * n * n * 4, transcendentals=n),
    )(a)


def shards(jacobian):
    row_count, par_width = jacobian.shape
    par_count = lax.axis_size("par")
    smp_count = lax.axis_size("smp")
    sample_total = row_count * smp_count
    param_total = par_width * par_count
    col_width = sample_total // par_count
    panel_piece = PANEL // par_count
    row_index = lax.axis_index("smp")
    col_index = lax.axis_index("par")
    f32 = jnp.float32

    gathered = lax.all_gather(jacobian, "smp", axis=0, tiled=True)
    widened = gathered.astype(f32)
    col_mean = jnp.sum(widened, axis=0) / sample_total
    centered = (widened - col_mean).astype(jnp.bfloat16)
    mine = lax.dynamic_slice_in_dim(centered, row_index * row_count, row_count, 0)
    head = centered[:PANEL]
    contract = (((1,), (1,)), ((), ()))

    main = lax.dot_general(centered, mine, contract, preferred_element_type=f32)
    square = lax.dot_general(head, head, contract, preferred_element_type=f32)
    band = lax.dot_general(centered, head, contract, preferred_element_type=f32)
    sq = centered.astype(f32)
    sumsq = jnp.sum(sq * sq)

    width = row_count
    panel_parts = jnp.concatenate(
        [
            main[:PANEL].reshape(par_count, panel_piece, width),
            square.reshape(par_count, panel_piece * PANEL // width, width),
            jnp.broadcast_to(sumsq, (par_count, 8, width)),
        ],
        axis=1,
    )
    chunk = panel_parts.shape[1]
    reduced = lax.psum_scatter(
        panel_parts.reshape(par_count * chunk, width), "par", scatter_dimension=0, tiled=True
    ) / param_total
    shared = lax.all_gather(reduced, "par", axis=0, tiled=False)

    main_parts = jnp.concatenate(
        [
            main.reshape(par_count, col_width, width),
            band.reshape(par_count, col_width * PANEL // width, width),
        ],
        axis=1,
    )
    main_parts, shared = lax.optimization_barrier((main_parts, shared))
    main_chunk = main_parts.shape[1]
    reduced_main = lax.psum_scatter(
        main_parts.reshape(par_count * main_chunk, width), "par", scatter_dimension=0, tiled=True
    ) / param_total
    tile = reduced_main[:col_width].T
    band_mine = reduced_main[col_width:].reshape(col_width, PANEL)

    o2 = panel_piece
    o3 = o2 + panel_piece * PANEL // width
    panel_t = shared[:, :o2].reshape(PANEL, width)
    square_g = shared[:, o2:o3].reshape(PANEL, PANEL)
    trace_total = shared[0, o3, 0]
    shift_value = shift_scale * trace_total / sample_total

    eye = jnp.arange(PANEL, dtype=jnp.int32)
    global_rows = row_index * row_count + jnp.arange(row_count, dtype=jnp.int32)
    global_cols = col_index * col_width + jnp.arange(col_width, dtype=jnp.int32)
    square_s = square_g + jnp.where(eye[:, None] == eye[None, :], shift_value, 0.0)
    panel_s = panel_t.T + jnp.where(global_rows[:, None] == eye[None, :], shift_value, 0.0)
    band_s = band_mine + jnp.where(global_cols[:, None] == eye[None, :], shift_value, 0.0)
    tile_s = tile + jnp.where(global_rows[:, None] == global_cols[None, :], shift_value, 0.0)

    _, inverse = chol_and_inverse(square_s)
    panel_out = lax.dot_general(panel_s, inverse, NT, precision=HI, preferred_element_type=f32)
    band_factor = lax.dot_general(inverse, band_s, NT, precision=HI, preferred_element_type=f32)
    schur_tile = tile_s - jnp.dot(panel_out, band_factor, precision=lax.Precision.HIGHEST)
    return (panel_out, schur_tile)


def solution(mesh):
    placed = (P("smp", "par"),)
    return jax.shard_map(
        shards,
        mesh=mesh,
        in_specs=placed,
        out_specs=(P("smp", None), P("smp", "par")),
        check_vma=False,
    )
```

```python
import functools

import jax
import jax.numpy as jnp
from jax import lax
from jax.experimental import pallas as pl
from jax.experimental.pallas import tpu as pltpu
from jax.sharding import PartitionSpec as P

PANEL = 512


shift_scale = 0.01


HI = lax.Precision.HIGHEST
NT = (((1,), (1,)), ((), ()))


def _chol_kernel(a_ref, l_ref, w_ref, s_ref, blk_a, blk_b, blk_lt, blk_w, *, n, b):
    nb = n // b
    f32 = jnp.float32
    s_ref[...] = a_ref[...]
    l_ref[...] = jnp.zeros((n, n), f32)
    w_ref[...] = jnp.zeros((n, n), f32)
    rows = lax.broadcasted_iota(jnp.int32, (b, b), 0)
    cols = lax.broadcasted_iota(jnp.int32, (b, b), 1)
    lane = lax.broadcasted_iota(jnp.int32, (1, b), 1)
    for k in range(nb):
        ks = pl.ds(k * b, b)
        blk_a[...] = s_ref[ks, ks]
        blk_b[...] = jnp.where(rows == cols, 1.0, 0.0).astype(f32)

        def step(j, carry):
            row = blk_a[pl.ds(j, 1), :]
            d = jnp.sum(jnp.where(lane == j, row, 0.0), axis=1, keepdims=True)
            s = jnp.sqrt(d)
            v_row = jnp.where(lane >= j, row / s, 0.0)
            v_col = jnp.transpose(jnp.broadcast_to(v_row, (8, b)))[:, 0:1]
            blk_a[...] = blk_a[...] - v_col * v_row
            x = blk_b[pl.ds(j, 1), :] / s
            blk_b[...] = blk_b[...] - v_col * x
            blk_lt[pl.ds(j, 1), :] = v_row
            blk_w[pl.ds(j, 1), :] = x
            return carry

        lax.fori_loop(0, b, step, 0)
        w_kk = blk_w[...]
        l_ref[ks, ks] = jnp.transpose(blk_lt[...])
        w_ref[ks, ks] = w_kk
        if k < nb - 1:
            rest = pl.ds((k + 1) * b, n - (k + 1) * b)
            below = lax.dot_general(s_ref[rest, ks], w_kk, NT, precision=HI, preferred_element_type=f32)
            l_ref[rest, ks] = below
            s_ref[rest, rest] = s_ref[rest, rest] - lax.dot_general(
                below, below, NT, precision=HI, preferred_element_type=f32
            )
    for i in range(1, nb):
        w_ii = w_ref[pl.ds(i * b, b), pl.ds(i * b, b)]
        for j in range(i):
            acc = jnp.zeros((b, b), f32)
            for m in range(j, i):
                acc = acc + jnp.dot(
                    l_ref[pl.ds(i * b, b), pl.ds(m * b, b)],
                    w_ref[pl.ds(m * b, b), pl.ds(j * b, b)],
                    precision=HI,
                    preferred_element_type=f32,
                )
            w_ref[pl.ds(i * b, b), pl.ds(j * b, b)] = -jnp.dot(
                w_ii, acc, precision=HI, preferred_element_type=f32
            )


def chol_and_inverse(a, block=128):
    n = a.shape[0]
    f32 = jnp.float32
    return pl.pallas_call(
        functools.partial(_chol_kernel, n=n, b=block),
        out_shape=(jax.ShapeDtypeStruct((n, n), f32), jax.ShapeDtypeStruct((n, n), f32)),
        in_specs=[pl.BlockSpec(memory_space=pltpu.VMEM)],
        out_specs=(pl.BlockSpec(memory_space=pltpu.VMEM), pl.BlockSpec(memory_space=pltpu.VMEM)),
        scratch_shapes=[
            pltpu.VMEM((n, n), f32),
            pltpu.VMEM((block, block), f32),
            pltpu.VMEM((block, block), f32),
            pltpu.VMEM((block, block), f32),
            pltpu.VMEM((block, block), f32),
        ],
        cost_estimate=pl.CostEstimate(flops=2 * n * n * n, bytes_accessed=3 * n * n * 4, transcendentals=n),
    )(a)


def shards(jacobian):
    row_count, par_width = jacobian.shape
    par_count = lax.axis_size("par")
    smp_count = lax.axis_size("smp")
    sample_total = row_count * smp_count
    param_total = par_width * par_count
    col_width = sample_total // par_count
    panel_piece = PANEL // par_count
    row_index = lax.axis_index("smp")
    col_index = lax.axis_index("par")
    f32 = jnp.float32

    gathered = lax.all_gather(jacobian, "smp", axis=0, tiled=True)
    widened = gathered.astype(f32)
    col_mean = jnp.sum(widened, axis=0) / sample_total
    centered = (widened - col_mean).astype(jnp.bfloat16)
    mine = lax.dynamic_slice_in_dim(centered, row_index * row_count, row_count, 0)
    head = centered[:PANEL]
    contract = (((1,), (1,)), ((), ()))

    main_t = lax.dot_general(mine, head, contract, preferred_element_type=f32)
    square = lax.dot_general(head, head, contract, preferred_element_type=f32)
    sq = centered.astype(f32)
    sumsq = jnp.sum(sq * sq)

    width = row_count
    panel_parts = jnp.concatenate(
        [
            main_t.T.reshape(par_count, panel_piece, width),
            square.reshape(par_count, panel_piece * PANEL // width, width),
            jnp.broadcast_to(sumsq, (par_count, 8, width)),
        ],
        axis=1,
    )
    chunk = panel_parts.shape[1]
    reduced = lax.psum_scatter(
        panel_parts.reshape(par_count * chunk, width), "par", scatter_dimension=0, tiled=True
    ) / param_total
    shared = lax.all_gather(reduced, "par", axis=0, tiled=False)

    lhs = jnp.concatenate([mine, head], axis=0)
    big = lax.dot_general(lhs, centered, contract, preferred_element_type=f32)
    big, shared = lax.optimization_barrier((big, shared))
    big = lax.psum_scatter(big, "par", scatter_dimension=1, tiled=True) / param_total
    tile = big[:row_count]
    band_t = big[row_count:]

    o2 = panel_piece
    o3 = o2 + panel_piece * PANEL // width
    panel_t = shared[:, :o2].reshape(PANEL, width)
    square_g = shared[:, o2:o3].reshape(PANEL, PANEL)
    trace_total = shared[0, o3, 0]
    shift_value = shift_scale * trace_total / sample_total

    eye = jnp.arange(PANEL, dtype=jnp.int32)
    global_rows = row_index * row_count + jnp.arange(row_count, dtype=jnp.int32)
    global_cols = col_index * col_width + jnp.arange(col_width, dtype=jnp.int32)
    square_s = square_g + jnp.where(eye[:, None] == eye[None, :], shift_value, 0.0)
    panel_s = panel_t.T + jnp.where(global_rows[:, None] == eye[None, :], shift_value, 0.0)
    band_s = band_t + jnp.where(eye[:, None] == global_cols[None, :], shift_value, 0.0)
    tile_s = tile + jnp.where(global_rows[:, None] == global_cols[None, :], shift_value, 0.0)

    _, inverse = chol_and_inverse(square_s)
    panel_out = lax.dot_general(panel_s, inverse, NT, precision=HI, preferred_element_type=f32)
    band_factor = jnp.dot(inverse, band_s, precision=HI, preferred_element_type=f32)
    schur_tile = tile_s - jnp.dot(panel_out, band_factor, precision=lax.Precision.HIGHEST)
    return (panel_out, schur_tile)


def solution(mesh):
    placed = (P("smp", "par"),)
    return jax.shard_map(
        shards,
        mesh=mesh,
        in_specs=placed,
        out_specs=(P("smp", None), P("smp", "par")),
        check_vma=False,
    )
```

```python
import functools

import jax
import jax.numpy as jnp
from jax import lax
from jax.experimental import pallas as pl
from jax.experimental.pallas import tpu as pltpu
from jax.sharding import PartitionSpec as P

PANEL = 512


shift_scale = 0.01


HI = lax.Precision.HIGHEST
NT = (((1,), (1,)), ((), ()))


def _chol_kernel(a_ref, l_ref, w_ref, s_ref, blk_a, blk_b, blk_lt, blk_w, *, n, b):
    nb = n // b
    f32 = jnp.float32
    s_ref[...] = a_ref[...]
    l_ref[...] = jnp.zeros((n, n), f32)
    w_ref[...] = jnp.zeros((n, n), f32)
    rows = lax.broadcasted_iota(jnp.int32, (b, b), 0)
    cols = lax.broadcasted_iota(jnp.int32, (b, b), 1)
    lane = lax.broadcasted_iota(jnp.int32, (1, b), 1)
    for k in range(nb):
        ks = pl.ds(k * b, b)
        blk_a[...] = s_ref[ks, ks]
        blk_b[...] = jnp.where(rows == cols, 1.0, 0.0).astype(f32)

        def step(j, carry):
            row = blk_a[pl.ds(j, 1), :]
            d = jnp.sum(jnp.where(lane == j, row, 0.0), axis=1, keepdims=True)
            s = jnp.sqrt(d)
            v_row = jnp.where(lane >= j, row / s, 0.0)
            v_col = jnp.transpose(jnp.broadcast_to(v_row, (8, b)))[:, 0:1]
            blk_a[...] = blk_a[...] - v_col * v_row
            x = blk_b[pl.ds(j, 1), :] / s
            blk_b[...] = blk_b[...] - v_col * x
            blk_lt[pl.ds(j, 1), :] = v_row
            blk_w[pl.ds(j, 1), :] = x
            return carry

        lax.fori_loop(0, b, step, 0)
        w_kk = blk_w[...]
        l_ref[ks, ks] = jnp.transpose(blk_lt[...])
        w_ref[ks, ks] = w_kk
        if k < nb - 1:
            rest = pl.ds((k + 1) * b, n - (k + 1) * b)
            below = lax.dot_general(s_ref[rest, ks], w_kk, NT, precision=HI, preferred_element_type=f32)
            l_ref[rest, ks] = below
            s_ref[rest, rest] = s_ref[rest, rest] - lax.dot_general(
                below, below, NT, precision=HI, preferred_element_type=f32
            )
    for i in range(1, nb):
        w_ii = w_ref[pl.ds(i * b, b), pl.ds(i * b, b)]
        for j in range(i):
            acc = jnp.zeros((b, b), f32)
            for m in range(j, i):
                acc = acc + jnp.dot(
                    l_ref[pl.ds(i * b, b), pl.ds(m * b, b)],
                    w_ref[pl.ds(m * b, b), pl.ds(j * b, b)],
                    precision=HI,
                    preferred_element_type=f32,
                )
            w_ref[pl.ds(i * b, b), pl.ds(j * b, b)] = -jnp.dot(
                w_ii, acc, precision=HI, preferred_element_type=f32
            )


def chol_and_inverse(a, block=128):
    n = a.shape[0]
    f32 = jnp.float32
    return pl.pallas_call(
        functools.partial(_chol_kernel, n=n, b=block),
        out_shape=(jax.ShapeDtypeStruct((n, n), f32), jax.ShapeDtypeStruct((n, n), f32)),
        in_specs=[pl.BlockSpec(memory_space=pltpu.VMEM)],
        out_specs=(pl.BlockSpec(memory_space=pltpu.VMEM), pl.BlockSpec(memory_space=pltpu.VMEM)),
        scratch_shapes=[
            pltpu.VMEM((n, n), f32),
            pltpu.VMEM((block, block), f32),
            pltpu.VMEM((block, block), f32),
            pltpu.VMEM((block, block), f32),
            pltpu.VMEM((block, block), f32),
        ],
        cost_estimate=pl.CostEstimate(flops=2 * n * n * n, bytes_accessed=3 * n * n * 4, transcendentals=n),
    )(a)


def reduce_by_halving(x, axis, count):
    index = lax.axis_index(axis)
    masks = [1 << k for k in range(count.bit_length() - 1)]
    masks = masks[:2] + masks[3:4] + masks[2:3] + masks[4:]
    size = x.shape[0]
    for mask in masks:
        half = size // 2
        bit = (index // mask) % 2
        keep = lax.dynamic_slice_in_dim(x, bit * half, half, 0)
        send = lax.dynamic_slice_in_dim(x, (1 - bit) * half, half, 0)
        x = keep + lax.ppermute(send, axis, [(i, i ^ mask) for i in range(count)])
        size = half
    for mask in reversed(masks):
        bit = (index // mask) % 2
        other = lax.ppermute(x, axis, [(i, i ^ mask) for i in range(count)])
        low = jnp.where(bit == 0, x, other)
        high = jnp.where(bit == 0, other, x)
        x = jnp.concatenate([low, high], axis=0)
    return x


def shards(jacobian):
    row_count, par_width = jacobian.shape
    par_count = lax.axis_size("par")
    smp_count = lax.axis_size("smp")
    sample_total = row_count * smp_count
    param_total = par_width * par_count
    col_width = sample_total // par_count
    panel_piece = PANEL // par_count
    row_index = lax.axis_index("smp")
    col_index = lax.axis_index("par")
    f32 = jnp.float32

    gathered = lax.all_gather(jacobian, "smp", axis=0, tiled=True)
    widened = gathered.astype(f32)
    col_mean = jnp.sum(widened, axis=0) / sample_total
    centered = (widened - col_mean).astype(jnp.bfloat16)
    mine = lax.dynamic_slice_in_dim(centered, row_index * row_count, row_count, 0)
    head = centered[:PANEL]
    contract = (((1,), (1,)), ((), ()))

    main_t = lax.dot_general(mine, head, contract, preferred_element_type=f32)
    square = lax.dot_general(head, head, contract, preferred_element_type=f32)
    sq = centered.astype(f32)
    sumsq = jnp.sum(sq * sq)

    fill = jnp.broadcast_to(sumsq, (row_count, PANEL))
    panel_in = jnp.concatenate([main_t, square, fill], axis=0)
    shared = reduce_by_halving(panel_in, "par", par_count) / param_total

    lhs = jnp.concatenate([mine, head], axis=0)
    big = lax.dot_general(lhs, centered, contract, preferred_element_type=f32)
    big, shared = lax.optimization_barrier((big, shared))
    big = lax.psum_scatter(big, "par", scatter_dimension=1, tiled=True) / param_total
    tile = big[:row_count]
    band_t = big[row_count:]

    panel_g = shared[:row_count]
    square_g = shared[row_count : row_count + PANEL]
    trace_total = shared[row_count + PANEL, 0]
    shift_value = shift_scale * trace_total / sample_total

    eye = jnp.arange(PANEL, dtype=jnp.int32)
    global_rows = row_index * row_count + jnp.arange(row_count, dtype=jnp.int32)
    global_cols = col_index * col_width + jnp.arange(col_width, dtype=jnp.int32)
    square_s = square_g + jnp.where(eye[:, None] == eye[None, :], shift_value, 0.0)
    panel_s = panel_g + jnp.where(global_rows[:, None] == eye[None, :], shift_value, 0.0)
    band_s = band_t + jnp.where(eye[:, None] == global_cols[None, :], shift_value, 0.0)
    tile_s = tile + jnp.where(global_rows[:, None] == global_cols[None, :], shift_value, 0.0)

    _, inverse = chol_and_inverse(square_s)
    panel_out = lax.dot_general(panel_s, inverse, NT, precision=HI, preferred_element_type=f32)
    band_factor = jnp.dot(inverse, band_s, precision=HI, preferred_element_type=f32)
    schur_tile = tile_s - jnp.dot(panel_out, band_factor, precision=lax.Precision.HIGHEST)
    return (panel_out, schur_tile)


def solution(mesh):
    placed = (P("smp", "par"),)
    return jax.shard_map(
        shards,
        mesh=mesh,
        in_specs=placed,
        out_specs=(P("smp", None), P("smp", "par")),
        check_vma=False,
    )
```

```python
import functools

import jax
import jax.numpy as jnp
from jax import lax
from jax.experimental import pallas as pl
from jax.experimental.pallas import tpu as pltpu
from jax.sharding import PartitionSpec as P

PANEL = 512


shift_scale = 0.01


HI = lax.Precision.HIGHEST
NT = (((1,), (1,)), ((), ()))


def _chol_kernel(a_ref, l_ref, w_ref, s_ref, blk_a, blk_b, blk_lt, blk_w, *, n, b):
    nb = n // b
    f32 = jnp.float32
    s_ref[...] = a_ref[...]
    l_ref[...] = jnp.zeros((n, n), f32)
    w_ref[...] = jnp.zeros((n, n), f32)
    rows = lax.broadcasted_iota(jnp.int32, (b, b), 0)
    cols = lax.broadcasted_iota(jnp.int32, (b, b), 1)
    lane = lax.broadcasted_iota(jnp.int32, (1, b), 1)
    sub = lax.broadcasted_iota(jnp.int32, (b, 1), 0)
    for k in range(nb):
        ks = pl.ds(k * b, b)
        blk_a[...] = s_ref[ks, ks]
        blk_b[...] = jnp.where(rows == cols, 1.0, 0.0).astype(f32)

        def step(j, carry):
            whole = blk_a[...]
            row = blk_a[pl.ds(j, 1), :]
            col = jnp.sum(jnp.where(cols == j, whole, 0.0), axis=1, keepdims=True)
            d = jnp.sum(jnp.where(lane == j, row, 0.0), axis=1, keepdims=True)
            r = 1.0 / jnp.sqrt(d)
            v_row = jnp.where(lane >= j, row * r, 0.0)
            v_col = jnp.where(sub >= j, col * r, 0.0)
            blk_a[...] = whole - v_col * v_row
            x = blk_b[pl.ds(j, 1), :] * r
            blk_b[...] = blk_b[...] - v_col * x
            blk_lt[pl.ds(j, 1), :] = v_row
            blk_w[pl.ds(j, 1), :] = x
            return carry

        lax.fori_loop(0, b, step, 0)
        w_kk = blk_w[...]
        l_ref[ks, ks] = jnp.transpose(blk_lt[...])
        w_ref[ks, ks] = w_kk
        if k < nb - 1:
            rest = pl.ds((k + 1) * b, n - (k + 1) * b)
            below = lax.dot_general(s_ref[rest, ks], w_kk, NT, precision=HI, preferred_element_type=f32)
            l_ref[rest, ks] = below
            s_ref[rest, rest] = s_ref[rest, rest] - lax.dot_general(
                below, below, NT, precision=HI, preferred_element_type=f32
            )
    for i in range(1, nb):
        w_ii = w_ref[pl.ds(i * b, b), pl.ds(i * b, b)]
        for j in range(i):
            acc = jnp.zeros((b, b), f32)
            for m in range(j, i):
                acc = acc + jnp.dot(
                    l_ref[pl.ds(i * b, b), pl.ds(m * b, b)],
                    w_ref[pl.ds(m * b, b), pl.ds(j * b, b)],
                    precision=HI,
                    preferred_element_type=f32,
                )
            w_ref[pl.ds(i * b, b), pl.ds(j * b, b)] = -jnp.dot(
                w_ii, acc, precision=HI, preferred_element_type=f32
            )


def chol_and_inverse(a, block=128):
    n = a.shape[0]
    f32 = jnp.float32
    return pl.pallas_call(
        functools.partial(_chol_kernel, n=n, b=block),
        out_shape=(jax.ShapeDtypeStruct((n, n), f32), jax.ShapeDtypeStruct((n, n), f32)),
        in_specs=[pl.BlockSpec(memory_space=pltpu.VMEM)],
        out_specs=(pl.BlockSpec(memory_space=pltpu.VMEM), pl.BlockSpec(memory_space=pltpu.VMEM)),
        scratch_shapes=[
            pltpu.VMEM((n, n), f32),
            pltpu.VMEM((block, block), f32),
            pltpu.VMEM((block, block), f32),
            pltpu.VMEM((block, block), f32),
            pltpu.VMEM((block, block), f32),
        ],
        cost_estimate=pl.CostEstimate(flops=2 * n * n * n, bytes_accessed=3 * n * n * 4, transcendentals=n),
    )(a)


def reduce_by_halving(x, axis, count):
    index = lax.axis_index(axis)
    masks = [1 << k for k in range(count.bit_length() - 1)]
    masks = masks[:2] + masks[3:4] + masks[2:3] + masks[4:]
    size = x.shape[0]
    for mask in masks:
        half = size // 2
        bit = (index // mask) % 2
        keep = lax.dynamic_slice_in_dim(x, bit * half, half, 0)
        send = lax.dynamic_slice_in_dim(x, (1 - bit) * half, half, 0)
        x = keep + lax.ppermute(send, axis, [(i, i ^ mask) for i in range(count)])
        size = half
    for mask in reversed(masks):
        bit = (index // mask) % 2
        other = lax.ppermute(x, axis, [(i, i ^ mask) for i in range(count)])
        low = jnp.where(bit == 0, x, other)
        high = jnp.where(bit == 0, other, x)
        x = jnp.concatenate([low, high], axis=0)
    return x


def shards(jacobian):
    row_count, par_width = jacobian.shape
    par_count = lax.axis_size("par")
    smp_count = lax.axis_size("smp")
    sample_total = row_count * smp_count
    param_total = par_width * par_count
    col_width = sample_total // par_count
    panel_piece = PANEL // par_count
    row_index = lax.axis_index("smp")
    col_index = lax.axis_index("par")
    f32 = jnp.float32

    gathered = lax.all_gather(jacobian, "smp", axis=0, tiled=True)
    widened = gathered.astype(f32)
    col_mean = jnp.sum(widened, axis=0) / sample_total
    centered = (widened - col_mean).astype(jnp.bfloat16)
    mine = lax.dynamic_slice_in_dim(centered, row_index * row_count, row_count, 0)
    head = centered[:PANEL]
    contract = (((1,), (1,)), ((), ()))

    main_t = lax.dot_general(mine, head, contract, preferred_element_type=f32)
    square = lax.dot_general(head, head, contract, preferred_element_type=f32)
    sq = centered.astype(f32)
    sumsq = jnp.sum(sq * sq)

    fill = jnp.broadcast_to(sumsq, (row_count, PANEL))
    panel_in = jnp.concatenate([main_t, square, fill], axis=0)
    shared = reduce_by_halving(panel_in, "par", par_count) / param_total

    lhs = jnp.concatenate([mine, head], axis=0)
    big = lax.dot_general(lhs, centered, contract, preferred_element_type=f32)
    big = lax.psum_scatter(big, "par", scatter_dimension=1, tiled=True) / param_total
    tile = big[:row_count]
    band_t = big[row_count:]

    panel_g = shared[:row_count]
    square_g = shared[row_count : row_count + PANEL]
    trace_total = shared[row_count + PANEL, 0]
    shift_value = shift_scale * trace_total / sample_total

    eye = jnp.arange(PANEL, dtype=jnp.int32)
    global_rows = row_index * row_count + jnp.arange(row_count, dtype=jnp.int32)
    global_cols = col_index * col_width + jnp.arange(col_width, dtype=jnp.int32)
    square_s = square_g + jnp.where(eye[:, None] == eye[None, :], shift_value, 0.0)
    panel_s = panel_g + jnp.where(global_rows[:, None] == eye[None, :], shift_value, 0.0)
    band_s = band_t + jnp.where(eye[:, None] == global_cols[None, :], shift_value, 0.0)
    tile_s = tile + jnp.where(global_rows[:, None] == global_cols[None, :], shift_value, 0.0)

    _, inverse = chol_and_inverse(square_s)
    panel_out = lax.dot_general(panel_s, inverse, NT, precision=HI, preferred_element_type=f32)
    band_factor = jnp.dot(inverse, band_s, precision=HI, preferred_element_type=f32)
    schur_tile = tile_s - jnp.dot(panel_out, band_factor, precision=lax.Precision.HIGHEST)
    return (panel_out, schur_tile)


def solution(mesh):
    placed = (P("smp", "par"),)
    return jax.shard_map(
        shards,
        mesh=mesh,
        in_specs=placed,
        out_specs=(P("smp", None), P("smp", "par")),
        check_vma=False,
    )
```

```python
import functools

import jax
import jax.numpy as jnp
from jax import lax
from jax.experimental import pallas as pl
from jax.experimental.pallas import tpu as pltpu
from jax.sharding import PartitionSpec as P

PANEL = 512


shift_scale = 0.01


HI = lax.Precision.HIGHEST
NT = (((1,), (1,)), ((), ()))


def _chol_kernel(a_ref, l_ref, w_ref, s_ref, blk_a, blk_b, blk_lt, blk_w, *, n, b):
    nb = n // b
    f32 = jnp.float32
    s_ref[...] = a_ref[...]
    l_ref[...] = jnp.zeros((n, n), f32)
    w_ref[...] = jnp.zeros((n, n), f32)
    rows = lax.broadcasted_iota(jnp.int32, (b, b), 0)
    cols = lax.broadcasted_iota(jnp.int32, (b, b), 1)
    lane = lax.broadcasted_iota(jnp.int32, (1, b), 1)
    sub = lax.broadcasted_iota(jnp.int32, (b, 1), 0)
    for k in range(nb):
        ks = pl.ds(k * b, b)
        blk_a[...] = s_ref[ks, ks]
        blk_b[...] = jnp.where(rows == cols, 1.0, 0.0).astype(f32)

        def step(j, carry):
            whole = blk_a[...]
            row = blk_a[pl.ds(j, 1), :]
            col = jnp.sum(jnp.where(cols == j, whole, 0.0), axis=1, keepdims=True)
            d = jnp.sum(jnp.where(lane == j, row, 0.0), axis=1, keepdims=True)
            r = lax.rsqrt(d)
            v_row = jnp.where(lane >= j, row * r, 0.0)
            v_col = jnp.where(sub >= j, col * r, 0.0)
            blk_a[...] = whole - v_col * v_row
            x = blk_b[pl.ds(j, 1), :] * r
            blk_b[...] = blk_b[...] - v_col * x
            blk_lt[pl.ds(j, 1), :] = v_row
            blk_w[pl.ds(j, 1), :] = x
            return carry

        lax.fori_loop(0, b, step, 0)
        w_kk = blk_w[...]
        l_ref[ks, ks] = jnp.transpose(blk_lt[...])
        w_ref[ks, ks] = w_kk
        if k < nb - 1:
            rest = pl.ds((k + 1) * b, n - (k + 1) * b)
            below = lax.dot_general(s_ref[rest, ks], w_kk, NT, precision=HI, preferred_element_type=f32)
            l_ref[rest, ks] = below
            s_ref[rest, rest] = s_ref[rest, rest] - lax.dot_general(
                below, below, NT, precision=HI, preferred_element_type=f32
            )
    for i in range(1, nb):
        w_ii = w_ref[pl.ds(i * b, b), pl.ds(i * b, b)]
        for j in range(i):
            acc = jnp.zeros((b, b), f32)
            for m in range(j, i):
                acc = acc + jnp.dot(
                    l_ref[pl.ds(i * b, b), pl.ds(m * b, b)],
                    w_ref[pl.ds(m * b, b), pl.ds(j * b, b)],
                    precision=HI,
                    preferred_element_type=f32,
                )
            w_ref[pl.ds(i * b, b), pl.ds(j * b, b)] = -jnp.dot(
                w_ii, acc, precision=HI, preferred_element_type=f32
            )


def chol_and_inverse(a, block=128):
    n = a.shape[0]
    f32 = jnp.float32
    return pl.pallas_call(
        functools.partial(_chol_kernel, n=n, b=block),
        out_shape=(jax.ShapeDtypeStruct((n, n), f32), jax.ShapeDtypeStruct((n, n), f32)),
        in_specs=[pl.BlockSpec(memory_space=pltpu.VMEM)],
        out_specs=(pl.BlockSpec(memory_space=pltpu.VMEM), pl.BlockSpec(memory_space=pltpu.VMEM)),
        scratch_shapes=[
            pltpu.VMEM((n, n), f32),
            pltpu.VMEM((block, block), f32),
            pltpu.VMEM((block, block), f32),
            pltpu.VMEM((block, block), f32),
            pltpu.VMEM((block, block), f32),
        ],
        cost_estimate=pl.CostEstimate(flops=2 * n * n * n, bytes_accessed=3 * n * n * 4, transcendentals=n),
    )(a)


def reduce_by_halving(x, axis, count):
    index = lax.axis_index(axis)
    masks = [1 << k for k in range(count.bit_length() - 1)]
    masks = masks[:2] + masks[3:4] + masks[2:3] + masks[4:]
    size = x.shape[0]
    for mask in masks:
        half = size // 2
        bit = (index // mask) % 2
        keep = lax.dynamic_slice_in_dim(x, bit * half, half, 0)
        send = lax.dynamic_slice_in_dim(x, (1 - bit) * half, half, 0)
        x = keep + lax.ppermute(send, axis, [(i, i ^ mask) for i in range(count)])
        size = half
    for mask in reversed(masks):
        bit = (index // mask) % 2
        other = lax.ppermute(x, axis, [(i, i ^ mask) for i in range(count)])
        low = jnp.where(bit == 0, x, other)
        high = jnp.where(bit == 0, other, x)
        x = jnp.concatenate([low, high], axis=0)
    return x


def shards(jacobian):
    row_count, par_width = jacobian.shape
    par_count = lax.axis_size("par")
    smp_count = lax.axis_size("smp")
    sample_total = row_count * smp_count
    param_total = par_width * par_count
    col_width = sample_total // par_count
    panel_piece = PANEL // par_count
    row_index = lax.axis_index("smp")
    col_index = lax.axis_index("par")
    f32 = jnp.float32

    gathered = lax.all_gather(jacobian, "smp", axis=0, tiled=True)
    widened = gathered.astype(f32)
    col_mean = jnp.sum(widened, axis=0) / sample_total
    centered = (widened - col_mean).astype(jnp.bfloat16)
    mine = lax.dynamic_slice_in_dim(centered, row_index * row_count, row_count, 0)
    head = centered[:PANEL]
    contract = (((1,), (1,)), ((), ()))

    main_t = lax.dot_general(mine, head, contract, preferred_element_type=f32)
    square = lax.dot_general(head, head, contract, preferred_element_type=f32)
    sq = centered.astype(f32)
    sumsq = jnp.sum(sq * sq)

    fill = jnp.broadcast_to(sumsq, (row_count, PANEL))
    panel_in = jnp.concatenate([main_t, square, fill], axis=0)
    shared = reduce_by_halving(panel_in, "par", par_count) / param_total

    lhs = jnp.concatenate([mine, head], axis=0)
    big = lax.dot_general(lhs, centered, contract, preferred_element_type=f32)
    big = lax.psum_scatter(big, "par", scatter_dimension=1, tiled=True) / param_total
    tile = big[:row_count]
    band_t = big[row_count:]

    panel_g = shared[:row_count]
    square_g = shared[row_count : row_count + PANEL]
    trace_total = shared[row_count + PANEL, 0]
    shift_value = shift_scale * trace_total / sample_total

    eye = jnp.arange(PANEL, dtype=jnp.int32)
    global_rows = row_index * row_count + jnp.arange(row_count, dtype=jnp.int32)
    global_cols = col_index * col_width + jnp.arange(col_width, dtype=jnp.int32)
    square_s = square_g + jnp.where(eye[:, None] == eye[None, :], shift_value, 0.0)
    panel_s = panel_g + jnp.where(global_rows[:, None] == eye[None, :], shift_value, 0.0)
    band_s = band_t + jnp.where(eye[:, None] == global_cols[None, :], shift_value, 0.0)
    tile_s = tile + jnp.where(global_rows[:, None] == global_cols[None, :], shift_value, 0.0)

    _, inverse = chol_and_inverse(square_s)
    panel_out = lax.dot_general(panel_s, inverse, NT, precision=HI, preferred_element_type=f32)
    band_factor = jnp.dot(inverse, band_s, precision=HI, preferred_element_type=f32)
    schur_tile = tile_s - jnp.dot(panel_out, band_factor, precision=lax.Precision.HIGHEST)
    return (panel_out, schur_tile)


def solution(mesh):
    placed = (P("smp", "par"),)
    return jax.shard_map(
        shards,
        mesh=mesh,
        in_specs=placed,
        out_specs=(P("smp", None), P("smp", "par")),
        check_vma=False,
    )
```

```python
import functools

import jax
import jax.numpy as jnp
from jax import lax
from jax.experimental import pallas as pl
from jax.experimental.pallas import tpu as pltpu
from jax.sharding import PartitionSpec as P

PANEL = 512


shift_scale = 0.01


HI = lax.Precision.HIGHEST
NT = (((1,), (1,)), ((), ()))


def _chol_kernel(a_ref, l_ref, w_ref, s_ref, blk_a, blk_b, blk_lt, blk_w, *, n, b):
    nb = n // b
    f32 = jnp.float32
    s_ref[...] = a_ref[...]
    l_ref[...] = jnp.zeros((n, n), f32)
    w_ref[...] = jnp.zeros((n, n), f32)
    rows = lax.broadcasted_iota(jnp.int32, (b, b), 0)
    cols = lax.broadcasted_iota(jnp.int32, (b, b), 1)
    lane = lax.broadcasted_iota(jnp.int32, (1, b), 1)
    sub = lax.broadcasted_iota(jnp.int32, (b, 1), 0)
    for k in range(nb):
        ks = pl.ds(k * b, b)
        blk_a[...] = s_ref[ks, ks]
        blk_b[...] = jnp.where(rows == cols, 1.0, 0.0).astype(f32)

        def step(j, carry):
            whole = blk_a[...]
            row = blk_a[pl.ds(j, 1), :]
            col = jnp.sum(jnp.where(cols == j, whole, 0.0), axis=1, keepdims=True)
            d = jnp.sum(jnp.where(lane == j, row, 0.0), axis=1, keepdims=True)
            r = lax.rsqrt(d)
            v_row = jnp.where(lane >= j, row * r, 0.0)
            v_col = jnp.where(sub >= j, col * r, 0.0)
            blk_a[...] = whole - v_col * v_row
            x = blk_b[pl.ds(j, 1), :] * r
            blk_b[...] = blk_b[...] - v_col * x
            blk_lt[pl.ds(j, 1), :] = v_row
            blk_w[pl.ds(j, 1), :] = x
            return carry

        lax.fori_loop(0, b, step, 0)
        w_kk = blk_w[...]
        l_ref[ks, ks] = jnp.transpose(blk_lt[...])
        w_ref[ks, ks] = w_kk
        if k < nb - 1:
            rest = pl.ds((k + 1) * b, n - (k + 1) * b)
            below = lax.dot_general(s_ref[rest, ks], w_kk, NT, precision=HI, preferred_element_type=f32)
            l_ref[rest, ks] = below
            s_ref[rest, rest] = s_ref[rest, rest] - lax.dot_general(
                below, below, NT, precision=HI, preferred_element_type=f32
            )
    for i in range(1, nb):
        w_ii = w_ref[pl.ds(i * b, b), pl.ds(i * b, b)]
        for j in range(i):
            acc = jnp.zeros((b, b), f32)
            for m in range(j, i):
                acc = acc + jnp.dot(
                    l_ref[pl.ds(i * b, b), pl.ds(m * b, b)],
                    w_ref[pl.ds(m * b, b), pl.ds(j * b, b)],
                    precision=HI,
                    preferred_element_type=f32,
                )
            w_ref[pl.ds(i * b, b), pl.ds(j * b, b)] = -jnp.dot(
                w_ii, acc, precision=HI, preferred_element_type=f32
            )


def chol_and_inverse(a, block=128):
    n = a.shape[0]
    f32 = jnp.float32
    return pl.pallas_call(
        functools.partial(_chol_kernel, n=n, b=block),
        out_shape=(jax.ShapeDtypeStruct((n, n), f32), jax.ShapeDtypeStruct((n, n), f32)),
        in_specs=[pl.BlockSpec(memory_space=pltpu.VMEM)],
        out_specs=(pl.BlockSpec(memory_space=pltpu.VMEM), pl.BlockSpec(memory_space=pltpu.VMEM)),
        scratch_shapes=[
            pltpu.VMEM((n, n), f32),
            pltpu.VMEM((block, block), f32),
            pltpu.VMEM((block, block), f32),
            pltpu.VMEM((block, block), f32),
            pltpu.VMEM((block, block), f32),
        ],
        cost_estimate=pl.CostEstimate(flops=2 * n * n * n, bytes_accessed=3 * n * n * 4, transcendentals=n),
    )(a)


def reduce_by_halving(x, axis, count):
    index = lax.axis_index(axis)
    core = index % 2
    rounds = [(1, 1), (2, 8), (8, 2), (4, 16), (16, 4)]
    size = x.shape[0]

    def partners(pair):
        return [(i, i ^ pair[i % 2]) for i in range(count)]

    def bit_of(pair):
        mask = jnp.where(core == 0, pair[0], pair[1])
        return (index // mask) % 2

    for pair in rounds:
        half = size // 2
        bit = bit_of(pair)
        keep = lax.dynamic_slice_in_dim(x, bit * half, half, 0)
        send = lax.dynamic_slice_in_dim(x, (1 - bit) * half, half, 0)
        x = keep + lax.ppermute(send, axis, partners(pair))
        size = half
    for pair in reversed(rounds):
        bit = bit_of(pair)
        other = lax.ppermute(x, axis, partners(pair))
        low = jnp.where(bit == 0, x, other)
        high = jnp.where(bit == 0, other, x)
        x = jnp.concatenate([low, high], axis=0)
    return x


def shards(jacobian):
    row_count, par_width = jacobian.shape
    par_count = lax.axis_size("par")
    smp_count = lax.axis_size("smp")
    sample_total = row_count * smp_count
    param_total = par_width * par_count
    col_width = sample_total // par_count
    panel_piece = PANEL // par_count
    row_index = lax.axis_index("smp")
    col_index = lax.axis_index("par")
    f32 = jnp.float32

    gathered = lax.all_gather(jacobian, "smp", axis=0, tiled=True)
    widened = gathered.astype(f32)
    col_mean = jnp.sum(widened, axis=0) / sample_total
    centered = (widened - col_mean).astype(jnp.bfloat16)
    mine = lax.dynamic_slice_in_dim(centered, row_index * row_count, row_count, 0)
    head = centered[:PANEL]
    contract = (((1,), (1,)), ((), ()))

    main_t = lax.dot_general(mine, head, contract, preferred_element_type=f32)
    square = lax.dot_general(head, head, contract, preferred_element_type=f32)
    sq = centered.astype(f32)
    sumsq = jnp.sum(sq * sq)

    fill = jnp.broadcast_to(sumsq, (row_count, PANEL))
    panel_in = jnp.concatenate([main_t, square, fill], axis=0)
    shared = reduce_by_halving(panel_in, "par", par_count) / param_total

    lhs = jnp.concatenate([mine, head], axis=0)
    big = lax.dot_general(lhs, centered, contract, preferred_element_type=f32)
    big = lax.psum_scatter(big, "par", scatter_dimension=1, tiled=True) / param_total
    tile = big[:row_count]
    band_t = big[row_count:]

    panel_g = shared[:row_count]
    square_g = shared[row_count : row_count + PANEL]
    trace_total = shared[row_count + PANEL, 0]
    shift_value = shift_scale * trace_total / sample_total

    eye = jnp.arange(PANEL, dtype=jnp.int32)
    global_rows = row_index * row_count + jnp.arange(row_count, dtype=jnp.int32)
    global_cols = col_index * col_width + jnp.arange(col_width, dtype=jnp.int32)
    square_s = square_g + jnp.where(eye[:, None] == eye[None, :], shift_value, 0.0)
    panel_s = panel_g + jnp.where(global_rows[:, None] == eye[None, :], shift_value, 0.0)
    band_s = band_t + jnp.where(eye[:, None] == global_cols[None, :], shift_value, 0.0)
    tile_s = tile + jnp.where(global_rows[:, None] == global_cols[None, :], shift_value, 0.0)

    _, inverse = chol_and_inverse(square_s)
    panel_out = lax.dot_general(panel_s, inverse, NT, precision=HI, preferred_element_type=f32)
    band_factor = jnp.dot(inverse, band_s, precision=HI, preferred_element_type=f32)
    schur_tile = tile_s - jnp.dot(panel_out, band_factor, precision=lax.Precision.HIGHEST)
    return (panel_out, schur_tile)


def solution(mesh):
    placed = (P("smp", "par"),)
    return jax.shard_map(
        shards,
        mesh=mesh,
        in_specs=placed,
        out_specs=(P("smp", None), P("smp", "par")),
        check_vma=False,
    )
```

```python
import functools

import jax
import jax.numpy as jnp
from jax import lax
from jax.experimental import pallas as pl
from jax.experimental.pallas import tpu as pltpu
from jax.sharding import PartitionSpec as P

PANEL = 512


shift_scale = 0.01


HI = lax.Precision.HIGHEST
NT = (((1,), (1,)), ((), ()))


def _chol_kernel(a_ref, l_ref, w_ref, s_ref, blk_a, blk_b, blk_lt, blk_w, *, n, b):
    nb = n // b
    f32 = jnp.float32
    whole = a_ref[...]
    lower = lax.broadcasted_iota(jnp.int32, (n, n), 0) >= lax.broadcasted_iota(jnp.int32, (n, n), 1)
    s_ref[...] = jnp.where(lower, whole, jnp.transpose(whole))
    l_ref[...] = jnp.zeros((n, n), f32)
    w_ref[...] = jnp.zeros((n, n), f32)
    rows = lax.broadcasted_iota(jnp.int32, (b, b), 0)
    cols = lax.broadcasted_iota(jnp.int32, (b, b), 1)
    lane = lax.broadcasted_iota(jnp.int32, (1, b), 1)
    sub = lax.broadcasted_iota(jnp.int32, (b, 1), 0)
    for k in range(nb):
        ks = pl.ds(k * b, b)
        blk_a[...] = s_ref[ks, ks]
        blk_b[...] = jnp.where(rows == cols, 1.0, 0.0).astype(f32)

        def step(j, carry):
            whole = blk_a[...]
            row = blk_a[pl.ds(j, 1), :]
            col = jnp.sum(jnp.where(cols == j, whole, 0.0), axis=1, keepdims=True)
            d = jnp.sum(jnp.where(lane == j, row, 0.0), axis=1, keepdims=True)
            r = lax.rsqrt(d)
            v_row = jnp.where(lane >= j, row * r, 0.0)
            v_col = jnp.where(sub >= j, col * r, 0.0)
            blk_a[...] = whole - v_col * v_row
            x = blk_b[pl.ds(j, 1), :] * r
            blk_b[...] = blk_b[...] - v_col * x
            blk_lt[pl.ds(j, 1), :] = v_row
            blk_w[pl.ds(j, 1), :] = x
            return carry

        lax.fori_loop(0, b, step, 0)
        w_kk = blk_w[...]
        l_ref[ks, ks] = jnp.transpose(blk_lt[...])
        w_ref[ks, ks] = w_kk
        if k < nb - 1:
            rest = pl.ds((k + 1) * b, n - (k + 1) * b)
            below = lax.dot_general(s_ref[rest, ks], w_kk, NT, precision=HI, preferred_element_type=f32)
            l_ref[rest, ks] = below
            s_ref[rest, rest] = s_ref[rest, rest] - lax.dot_general(
                below, below, NT, precision=HI, preferred_element_type=f32
            )
    for i in range(1, nb):
        w_ii = w_ref[pl.ds(i * b, b), pl.ds(i * b, b)]
        for j in range(i):
            acc = jnp.zeros((b, b), f32)
            for m in range(j, i):
                acc = acc + jnp.dot(
                    l_ref[pl.ds(i * b, b), pl.ds(m * b, b)],
                    w_ref[pl.ds(m * b, b), pl.ds(j * b, b)],
                    precision=HI,
                    preferred_element_type=f32,
                )
            w_ref[pl.ds(i * b, b), pl.ds(j * b, b)] = -jnp.dot(
                w_ii, acc, precision=HI, preferred_element_type=f32
            )


def chol_and_inverse(a, block=128):
    n = a.shape[0]
    f32 = jnp.float32
    return pl.pallas_call(
        functools.partial(_chol_kernel, n=n, b=block),
        out_shape=(jax.ShapeDtypeStruct((n, n), f32), jax.ShapeDtypeStruct((n, n), f32)),
        in_specs=[pl.BlockSpec(memory_space=pltpu.VMEM)],
        out_specs=(pl.BlockSpec(memory_space=pltpu.VMEM), pl.BlockSpec(memory_space=pltpu.VMEM)),
        scratch_shapes=[
            pltpu.VMEM((n, n), f32),
            pltpu.VMEM((block, block), f32),
            pltpu.VMEM((block, block), f32),
            pltpu.VMEM((block, block), f32),
            pltpu.VMEM((block, block), f32),
        ],
        cost_estimate=pl.CostEstimate(flops=2 * n * n * n, bytes_accessed=3 * n * n * 4, transcendentals=n),
    )(a)


def reduce_by_halving(x, axis, count):
    index = lax.axis_index(axis)
    core = index % 2
    rounds = [(1, 1), (2, 8), (8, 2), (4, 16), (16, 4)]
    size = x.shape[0]

    def partners(pair):
        return [(i, i ^ pair[i % 2]) for i in range(count)]

    def bit_of(pair):
        mask = jnp.where(core == 0, pair[0], pair[1])
        return (index // mask) % 2

    for pair in rounds:
        half = size // 2
        bit = bit_of(pair)
        keep = lax.dynamic_slice_in_dim(x, bit * half, half, 0)
        send = lax.dynamic_slice_in_dim(x, (1 - bit) * half, half, 0)
        x = keep + lax.ppermute(send, axis, partners(pair))
        size = half
    for pair in reversed(rounds):
        bit = bit_of(pair)
        other = lax.ppermute(x, axis, partners(pair))
        low = jnp.where(bit == 0, x, other)
        high = jnp.where(bit == 0, other, x)
        x = jnp.concatenate([low, high], axis=0)
    return x


def shards(jacobian):
    row_count, par_width = jacobian.shape
    par_count = lax.axis_size("par")
    smp_count = lax.axis_size("smp")
    sample_total = row_count * smp_count
    param_total = par_width * par_count
    col_width = sample_total // par_count
    panel_piece = PANEL // par_count
    row_index = lax.axis_index("smp")
    col_index = lax.axis_index("par")
    f32 = jnp.float32

    gathered = lax.all_gather(jacobian, "smp", axis=0, tiled=True)
    widened = gathered.astype(f32)
    col_mean = jnp.sum(widened, axis=0) / sample_total
    centered = (widened - col_mean).astype(jnp.bfloat16)
    mine = lax.dynamic_slice_in_dim(centered, row_index * row_count, row_count, 0)
    head = centered[:PANEL]
    contract = (((1,), (1,)), ((), ()))

    main_t = lax.dot_general(mine, head, contract, preferred_element_type=f32)
    square = lax.dot_general(head, head, contract, preferred_element_type=f32)
    sq = centered.astype(f32)
    sumsq = jnp.sum(sq * sq)

    corner = (jnp.arange(PANEL)[:, None] == 0) & (jnp.arange(PANEL)[None, :] == PANEL - 1)
    square = jnp.where(corner, sumsq, square)
    panel_in = jnp.concatenate([main_t, square], axis=0)
    shared = reduce_by_halving(panel_in, "par", par_count) / param_total

    lhs = jnp.concatenate([mine, head], axis=0)
    big = lax.dot_general(lhs, centered, contract, preferred_element_type=f32)
    big = lax.psum_scatter(big, "par", scatter_dimension=1, tiled=True) / param_total
    tile = big[:row_count]
    band_t = big[row_count:]

    panel_g = shared[:row_count]
    square_g = shared[row_count : row_count + PANEL]
    trace_total = shared[row_count, PANEL - 1]
    shift_value = shift_scale * trace_total / sample_total

    eye = jnp.arange(PANEL, dtype=jnp.int32)
    global_rows = row_index * row_count + jnp.arange(row_count, dtype=jnp.int32)
    global_cols = col_index * col_width + jnp.arange(col_width, dtype=jnp.int32)
    square_s = square_g + jnp.where(eye[:, None] == eye[None, :], shift_value, 0.0)
    panel_s = panel_g + jnp.where(global_rows[:, None] == eye[None, :], shift_value, 0.0)
    band_s = band_t + jnp.where(eye[:, None] == global_cols[None, :], shift_value, 0.0)
    tile_s = tile + jnp.where(global_rows[:, None] == global_cols[None, :], shift_value, 0.0)

    _, inverse = chol_and_inverse(square_s)
    panel_out = lax.dot_general(panel_s, inverse, NT, precision=HI, preferred_element_type=f32)
    band_factor = jnp.dot(inverse, band_s, precision=HI, preferred_element_type=f32)
    schur_tile = tile_s - jnp.dot(panel_out, band_factor, precision=lax.Precision.HIGHEST)
    return (panel_out, schur_tile)


def solution(mesh):
    placed = (P("smp", "par"),)
    return jax.shard_map(
        shards,
        mesh=mesh,
        in_specs=placed,
        out_specs=(P("smp", None), P("smp", "par")),
        check_vma=False,
    )
```

```python
import functools

import jax
import jax.numpy as jnp
from jax import lax
from jax.experimental import pallas as pl
from jax.experimental.pallas import tpu as pltpu
from jax.sharding import PartitionSpec as P

PANEL = 512


shift_scale = 0.01


HI = lax.Precision.HIGHEST
NT = (((1,), (1,)), ((), ()))


def _chol_kernel(a_ref, l_ref, w_ref, s_ref, blk_a, blk_b, blk_lt, blk_w, *, n, b):
    nb = n // b
    f32 = jnp.float32
    whole = a_ref[...]
    lower = lax.broadcasted_iota(jnp.int32, (n, n), 0) >= lax.broadcasted_iota(jnp.int32, (n, n), 1)
    s_ref[...] = jnp.where(lower, whole, jnp.transpose(whole))
    l_ref[...] = jnp.zeros((n, n), f32)
    w_ref[...] = jnp.zeros((n, n), f32)
    rows = lax.broadcasted_iota(jnp.int32, (b, b), 0)
    cols = lax.broadcasted_iota(jnp.int32, (b, b), 1)
    lane = lax.broadcasted_iota(jnp.int32, (1, b), 1)
    sub = lax.broadcasted_iota(jnp.int32, (b, 1), 0)
    for k in range(nb):
        ks = pl.ds(k * b, b)
        blk_a[...] = s_ref[ks, ks]
        blk_b[...] = jnp.where(rows == cols, 1.0, 0.0).astype(f32)

        def step(j, carry):
            whole = blk_a[...]
            row = blk_a[pl.ds(j, 1), :]
            col = jnp.sum(jnp.where(cols == j, whole, 0.0), axis=1, keepdims=True)
            d = jnp.sum(jnp.where(lane == j, row, 0.0), axis=1, keepdims=True)
            r = lax.rsqrt(d)
            v_row = jnp.where(lane >= j, row * r, 0.0)
            v_col = jnp.where(sub >= j, col * r, 0.0)
            blk_a[...] = whole - v_col * v_row
            x = blk_b[pl.ds(j, 1), :] * r
            blk_b[...] = blk_b[...] - v_col * x
            blk_lt[pl.ds(j, 1), :] = v_row
            blk_w[pl.ds(j, 1), :] = x
            return carry

        lax.fori_loop(0, b, step, 0)
        w_kk = blk_w[...]
        l_ref[ks, ks] = jnp.transpose(blk_lt[...])
        w_ref[ks, ks] = w_kk
        if k < nb - 1:
            rest = pl.ds((k + 1) * b, n - (k + 1) * b)
            below = lax.dot_general(s_ref[rest, ks], w_kk, NT, precision=HI, preferred_element_type=f32)
            l_ref[rest, ks] = below
            s_ref[rest, rest] = s_ref[rest, rest] - lax.dot_general(
                below, below, NT, precision=HI, preferred_element_type=f32
            )
    for i in range(1, nb):
        w_ii = w_ref[pl.ds(i * b, b), pl.ds(i * b, b)]
        for j in range(i):
            acc = jnp.zeros((b, b), f32)
            for m in range(j, i):
                acc = acc + jnp.dot(
                    l_ref[pl.ds(i * b, b), pl.ds(m * b, b)],
                    w_ref[pl.ds(m * b, b), pl.ds(j * b, b)],
                    precision=HI,
                    preferred_element_type=f32,
                )
            w_ref[pl.ds(i * b, b), pl.ds(j * b, b)] = -jnp.dot(
                w_ii, acc, precision=HI, preferred_element_type=f32
            )


def chol_and_inverse(a, block=128):
    n = a.shape[0]
    f32 = jnp.float32
    return pl.pallas_call(
        functools.partial(_chol_kernel, n=n, b=block),
        out_shape=(jax.ShapeDtypeStruct((n, n), f32), jax.ShapeDtypeStruct((n, n), f32)),
        in_specs=[pl.BlockSpec(memory_space=pltpu.VMEM)],
        out_specs=(pl.BlockSpec(memory_space=pltpu.VMEM), pl.BlockSpec(memory_space=pltpu.VMEM)),
        scratch_shapes=[
            pltpu.VMEM((n, n), f32),
            pltpu.VMEM((block, block), f32),
            pltpu.VMEM((block, block), f32),
            pltpu.VMEM((block, block), f32),
            pltpu.VMEM((block, block), f32),
        ],
        cost_estimate=pl.CostEstimate(flops=2 * n * n * n, bytes_accessed=3 * n * n * 4, transcendentals=n),
    )(a)


def reduce_by_halving(x, axis, count):
    index = lax.axis_index(axis)
    core = index % 2
    halving = [(1, 1), (2, 8)]
    doubling = [(8, 2), (4, 16), (16, 4)]
    size = x.shape[0]

    def partners(pair):
        return [(i, i ^ pair[i % 2]) for i in range(count)]

    def bit_of(pair):
        mask = jnp.where(core == 0, pair[0], pair[1])
        return (index // mask) % 2

    for pair in halving:
        half = size // 2
        bit = bit_of(pair)
        keep = lax.dynamic_slice_in_dim(x, bit * half, half, 0)
        send = lax.dynamic_slice_in_dim(x, (1 - bit) * half, half, 0)
        x = keep + lax.ppermute(send, axis, partners(pair))
        size = half
    for pair in doubling:
        x = x + lax.ppermute(x, axis, partners(pair))
    for pair in reversed(halving):
        bit = bit_of(pair)
        other = lax.ppermute(x, axis, partners(pair))
        low = jnp.where(bit == 0, x, other)
        high = jnp.where(bit == 0, other, x)
        x = jnp.concatenate([low, high], axis=0)
    return x


def shards(jacobian):
    row_count, par_width = jacobian.shape
    par_count = lax.axis_size("par")
    smp_count = lax.axis_size("smp")
    sample_total = row_count * smp_count
    param_total = par_width * par_count
    col_width = sample_total // par_count
    panel_piece = PANEL // par_count
    row_index = lax.axis_index("smp")
    col_index = lax.axis_index("par")
    f32 = jnp.float32

    gathered = lax.all_gather(jacobian, "smp", axis=0, tiled=True)
    widened = gathered.astype(f32)
    col_mean = jnp.sum(widened, axis=0) / sample_total
    centered = (widened - col_mean).astype(jnp.bfloat16)
    mine = lax.dynamic_slice_in_dim(centered, row_index * row_count, row_count, 0)
    head = centered[:PANEL]
    contract = (((1,), (1,)), ((), ()))

    main_t = lax.dot_general(mine, head, contract, preferred_element_type=f32)
    square = lax.dot_general(head, head, contract, preferred_element_type=f32)
    sq = centered.astype(f32)
    sumsq = jnp.sum(sq * sq)

    corner = (jnp.arange(PANEL)[:, None] == 0) & (jnp.arange(PANEL)[None, :] == PANEL - 1)
    square = jnp.where(corner, sumsq, square)
    panel_in = jnp.concatenate([main_t, square], axis=0)
    shared = reduce_by_halving(panel_in, "par", par_count) / param_total

    lhs = jnp.concatenate([mine, head], axis=0)
    big = lax.dot_general(lhs, centered, contract, preferred_element_type=f32)
    big = lax.psum_scatter(big, "par", scatter_dimension=1, tiled=True) / param_total
    tile = big[:row_count]
    band_t = big[row_count:]

    panel_g = shared[:row_count]
    square_g = shared[row_count : row_count + PANEL]
    trace_total = shared[row_count, PANEL - 1]
    shift_value = shift_scale * trace_total / sample_total

    eye = jnp.arange(PANEL, dtype=jnp.int32)
    global_rows = row_index * row_count + jnp.arange(row_count, dtype=jnp.int32)
    global_cols = col_index * col_width + jnp.arange(col_width, dtype=jnp.int32)
    square_s = square_g + jnp.where(eye[:, None] == eye[None, :], shift_value, 0.0)
    panel_s = panel_g + jnp.where(global_rows[:, None] == eye[None, :], shift_value, 0.0)
    band_s = band_t + jnp.where(eye[:, None] == global_cols[None, :], shift_value, 0.0)
    tile_s = tile + jnp.where(global_rows[:, None] == global_cols[None, :], shift_value, 0.0)

    _, inverse = chol_and_inverse(square_s)
    panel_out = lax.dot_general(panel_s, inverse, NT, precision=HI, preferred_element_type=f32)
    band_factor = jnp.dot(inverse, band_s, precision=HI, preferred_element_type=f32)
    schur_tile = tile_s - jnp.dot(panel_out, band_factor, precision=lax.Precision.HIGHEST)
    return (panel_out, schur_tile)


def solution(mesh):
    placed = (P("smp", "par"),)
    return jax.shard_map(
        shards,
        mesh=mesh,
        in_specs=placed,
        out_specs=(P("smp", None), P("smp", "par")),
        check_vma=False,
    )
```

```python
import functools

import jax
import jax.numpy as jnp
from jax import lax
from jax.experimental import pallas as pl
from jax.experimental.pallas import tpu as pltpu
from jax.sharding import PartitionSpec as P

PANEL = 512


shift_scale = 0.01


HI = lax.Precision.HIGHEST
NT = (((1,), (1,)), ((), ()))


def _chol_kernel(a_ref, p_ref, po_ref, p2_ref, l_ref, w_ref, s_ref, blk_a, blk_b, blk_lt, blk_w, *, n, b):
    nb = n // b
    f32 = jnp.float32
    whole = a_ref[...]
    lower = lax.broadcasted_iota(jnp.int32, (n, n), 0) >= lax.broadcasted_iota(jnp.int32, (n, n), 1)
    s_ref[...] = jnp.where(lower, whole, jnp.transpose(whole))
    l_ref[...] = jnp.zeros((n, n), f32)
    w_ref[...] = jnp.zeros((n, n), f32)
    rows = lax.broadcasted_iota(jnp.int32, (b, b), 0)
    cols = lax.broadcasted_iota(jnp.int32, (b, b), 1)
    lane = lax.broadcasted_iota(jnp.int32, (1, b), 1)
    sub = lax.broadcasted_iota(jnp.int32, (b, 1), 0)
    for k in range(nb):
        ks = pl.ds(k * b, b)
        blk_a[...] = s_ref[ks, ks]
        blk_b[...] = jnp.where(rows == cols, 1.0, 0.0).astype(f32)

        def step(j, carry):
            whole = blk_a[...]
            row = blk_a[pl.ds(j, 1), :]
            col = jnp.sum(jnp.where(cols == j, whole, 0.0), axis=1, keepdims=True)
            d = jnp.sum(jnp.where(lane == j, row, 0.0), axis=1, keepdims=True)
            r = lax.rsqrt(d)
            v_row = jnp.where(lane >= j, row * r, 0.0)
            v_col = jnp.where(sub >= j, col * r, 0.0)
            blk_a[...] = whole - v_col * v_row
            x = blk_b[pl.ds(j, 1), :] * r
            blk_b[...] = blk_b[...] - v_col * x
            blk_lt[pl.ds(j, 1), :] = v_row
            blk_w[pl.ds(j, 1), :] = x
            return carry

        lax.fori_loop(0, b, step, 0)
        w_kk = blk_w[...]
        l_ref[ks, ks] = jnp.transpose(blk_lt[...])
        w_ref[ks, ks] = w_kk
        if k < nb - 1:
            rest = pl.ds((k + 1) * b, n - (k + 1) * b)
            below = lax.dot_general(s_ref[rest, ks], w_kk, NT, precision=HI, preferred_element_type=f32)
            l_ref[rest, ks] = below
            s_ref[rest, rest] = s_ref[rest, rest] - lax.dot_general(
                below, below, NT, precision=HI, preferred_element_type=f32
            )
    for i in range(1, nb):
        w_ii = w_ref[pl.ds(i * b, b), pl.ds(i * b, b)]
        for j in range(i):
            acc = jnp.zeros((b, b), f32)
            for m in range(j, i):
                acc = acc + jnp.dot(
                    l_ref[pl.ds(i * b, b), pl.ds(m * b, b)],
                    w_ref[pl.ds(m * b, b), pl.ds(j * b, b)],
                    precision=HI,
                    preferred_element_type=f32,
                )
            w_ref[pl.ds(i * b, b), pl.ds(j * b, b)] = -jnp.dot(
                w_ii, acc, precision=HI, preferred_element_type=f32
            )
    inverse = w_ref[...]
    panel_out = lax.dot_general(p_ref[...], inverse, NT, precision=HI, preferred_element_type=f32)
    po_ref[...] = panel_out
    p2_ref[...] = jnp.dot(panel_out, inverse, precision=HI, preferred_element_type=f32)


def chol_and_inverse(a, panel, block=128):
    n = a.shape[0]
    f32 = jnp.float32
    vmem = pl.BlockSpec(memory_space=pltpu.VMEM)
    return pl.pallas_call(
        functools.partial(_chol_kernel, n=n, b=block),
        out_shape=(jax.ShapeDtypeStruct(panel.shape, f32), jax.ShapeDtypeStruct(panel.shape, f32)),
        in_specs=[vmem, vmem],
        out_specs=(vmem, vmem),
        scratch_shapes=[
            pltpu.VMEM((n, n), f32),
            pltpu.VMEM((n, n), f32),
            pltpu.VMEM((n, n), f32),
            pltpu.VMEM((block, block), f32),
            pltpu.VMEM((block, block), f32),
            pltpu.VMEM((block, block), f32),
            pltpu.VMEM((block, block), f32),
        ],
        cost_estimate=pl.CostEstimate(
            flops=2 * n * n * n + 4 * panel.shape[0] * n * n, bytes_accessed=5 * n * n * 4, transcendentals=n
        ),
    )(a, panel)


def reduce_by_halving(x, axis, count):
    index = lax.axis_index(axis)
    core = index % 2
    halving = [(1, 1), (2, 8)]
    doubling = [(8, 2), (4, 16), (16, 4)]
    size = x.shape[0]

    def partners(pair):
        return [(i, i ^ pair[i % 2]) for i in range(count)]

    def bit_of(pair):
        mask = jnp.where(core == 0, pair[0], pair[1])
        return (index // mask) % 2

    for pair in halving:
        half = size // 2
        bit = bit_of(pair)
        keep = lax.dynamic_slice_in_dim(x, bit * half, half, 0)
        send = lax.dynamic_slice_in_dim(x, (1 - bit) * half, half, 0)
        x = keep + lax.ppermute(send, axis, partners(pair))
        size = half
    for pair in doubling:
        x = x + lax.ppermute(x, axis, partners(pair))
    for pair in reversed(halving):
        bit = bit_of(pair)
        other = lax.ppermute(x, axis, partners(pair))
        low = jnp.where(bit == 0, x, other)
        high = jnp.where(bit == 0, other, x)
        x = jnp.concatenate([low, high], axis=0)
    return x


def shards(jacobian):
    row_count, par_width = jacobian.shape
    par_count = lax.axis_size("par")
    smp_count = lax.axis_size("smp")
    sample_total = row_count * smp_count
    param_total = par_width * par_count
    col_width = sample_total // par_count
    panel_piece = PANEL // par_count
    row_index = lax.axis_index("smp")
    col_index = lax.axis_index("par")
    f32 = jnp.float32

    gathered = lax.all_gather(jacobian, "smp", axis=0, tiled=True)
    widened = gathered.astype(f32)
    col_mean = jnp.sum(widened, axis=0) / sample_total
    centered = (widened - col_mean).astype(jnp.bfloat16)
    mine = lax.dynamic_slice_in_dim(centered, row_index * row_count, row_count, 0)
    head = centered[:PANEL]
    contract = (((1,), (1,)), ((), ()))

    main_t = lax.dot_general(mine, head, contract, preferred_element_type=f32)
    square = lax.dot_general(head, head, contract, preferred_element_type=f32)
    sq = centered.astype(f32)
    sumsq = jnp.sum(sq * sq)

    corner = (jnp.arange(PANEL)[:, None] == 0) & (jnp.arange(PANEL)[None, :] == PANEL - 1)
    square = jnp.where(corner, sumsq, square)
    panel_in = jnp.concatenate([main_t, square], axis=0)
    shared = reduce_by_halving(panel_in, "par", par_count) / param_total

    lhs = jnp.concatenate([mine, head], axis=0)
    big = lax.dot_general(lhs, centered, contract, preferred_element_type=f32)
    big = lax.psum_scatter(big, "par", scatter_dimension=1, tiled=True) / param_total
    tile = big[:row_count]
    band_t = big[row_count:]

    panel_g = shared[:row_count]
    square_g = shared[row_count : row_count + PANEL]
    trace_total = shared[row_count, PANEL - 1]
    shift_value = shift_scale * trace_total / sample_total

    eye = jnp.arange(PANEL, dtype=jnp.int32)
    global_rows = row_index * row_count + jnp.arange(row_count, dtype=jnp.int32)
    global_cols = col_index * col_width + jnp.arange(col_width, dtype=jnp.int32)
    square_s = square_g + jnp.where(eye[:, None] == eye[None, :], shift_value, 0.0)
    panel_s = panel_g + jnp.where(global_rows[:, None] == eye[None, :], shift_value, 0.0)
    band_s = band_t + jnp.where(eye[:, None] == global_cols[None, :], shift_value, 0.0)
    tile_s = tile + jnp.where(global_rows[:, None] == global_cols[None, :], shift_value, 0.0)

    panel_out, projected = chol_and_inverse(square_s, panel_s)
    schur_tile = tile_s - jnp.dot(projected, band_s, precision=HI, preferred_element_type=f32)
    return (panel_out, schur_tile)


def solution(mesh):
    placed = (P("smp", "par"),)
    return jax.shard_map(
        shards,
        mesh=mesh,
        in_specs=placed,
        out_specs=(P("smp", None), P("smp", "par")),
        check_vma=False,
    )
```

```python
import functools

import jax
import jax.numpy as jnp
from jax import lax
from jax.experimental import pallas as pl
from jax.experimental.pallas import tpu as pltpu
from jax.sharding import PartitionSpec as P

PANEL = 512


shift_scale = 0.01


HI = lax.Precision.HIGHEST
NT = (((1,), (1,)), ((), ()))


def lower_blocks(count):
    return [(i, j) for i in range(count) for j in range(i + 1)]


def _chol_kernel(a_ref, p_ref, po_ref, p2_ref, l_ref, w_ref, s_ref, blk_a, blk_b, blk_lt, blk_w, *, n, b):
    nb = n // b
    f32 = jnp.float32
    lower = lax.broadcasted_iota(jnp.int32, (b, b), 0) >= lax.broadcasted_iota(jnp.int32, (b, b), 1)
    per_group = n // b
    for idx, (i, j) in enumerate(lower_blocks(n // b)):
        g, c = divmod(idx, per_group)
        blk = a_ref[pl.ds(g * b, b), pl.ds(c * b, b)]
        if i == j:
            s_ref[pl.ds(i * b, b), pl.ds(i * b, b)] = jnp.where(lower, blk, jnp.transpose(blk))
        else:
            s_ref[pl.ds(i * b, b), pl.ds(j * b, b)] = blk
            s_ref[pl.ds(j * b, b), pl.ds(i * b, b)] = jnp.transpose(blk)
    l_ref[...] = jnp.zeros((n, n), f32)
    w_ref[...] = jnp.zeros((n, n), f32)
    rows = lax.broadcasted_iota(jnp.int32, (b, b), 0)
    cols = lax.broadcasted_iota(jnp.int32, (b, b), 1)
    lane = lax.broadcasted_iota(jnp.int32, (1, b), 1)
    sub = lax.broadcasted_iota(jnp.int32, (b, 1), 0)
    for k in range(nb):
        ks = pl.ds(k * b, b)
        blk_a[...] = s_ref[ks, ks]
        blk_b[...] = jnp.where(rows == cols, 1.0, 0.0).astype(f32)

        def step(j, carry):
            whole = blk_a[...]
            row = blk_a[pl.ds(j, 1), :]
            col = jnp.sum(jnp.where(cols == j, whole, 0.0), axis=1, keepdims=True)
            d = jnp.sum(jnp.where(lane == j, row, 0.0), axis=1, keepdims=True)
            r = lax.rsqrt(d)
            v_row = jnp.where(lane >= j, row * r, 0.0)
            v_col = jnp.where(sub >= j, col * r, 0.0)
            blk_a[...] = whole - v_col * v_row
            x = blk_b[pl.ds(j, 1), :] * r
            blk_b[...] = blk_b[...] - v_col * x
            blk_lt[pl.ds(j, 1), :] = v_row
            blk_w[pl.ds(j, 1), :] = x
            return carry

        lax.fori_loop(0, b, step, 0)
        w_kk = blk_w[...]
        l_ref[ks, ks] = jnp.transpose(blk_lt[...])
        w_ref[ks, ks] = w_kk
        if k < nb - 1:
            rest = pl.ds((k + 1) * b, n - (k + 1) * b)
            below = lax.dot_general(s_ref[rest, ks], w_kk, NT, precision=HI, preferred_element_type=f32)
            l_ref[rest, ks] = below
            s_ref[rest, rest] = s_ref[rest, rest] - lax.dot_general(
                below, below, NT, precision=HI, preferred_element_type=f32
            )
    for i in range(1, nb):
        w_ii = w_ref[pl.ds(i * b, b), pl.ds(i * b, b)]
        for j in range(i):
            acc = jnp.zeros((b, b), f32)
            for m in range(j, i):
                acc = acc + jnp.dot(
                    l_ref[pl.ds(i * b, b), pl.ds(m * b, b)],
                    w_ref[pl.ds(m * b, b), pl.ds(j * b, b)],
                    precision=HI,
                    preferred_element_type=f32,
                )
            w_ref[pl.ds(i * b, b), pl.ds(j * b, b)] = -jnp.dot(
                w_ii, acc, precision=HI, preferred_element_type=f32
            )
    inverse = w_ref[...]
    panel_out = lax.dot_general(p_ref[...], inverse, NT, precision=HI, preferred_element_type=f32)
    po_ref[...] = panel_out
    p2_ref[...] = jnp.dot(panel_out, inverse, precision=HI, preferred_element_type=f32)


def chol_and_inverse(a, panel, block=128):
    n = panel.shape[1]
    f32 = jnp.float32
    vmem = pl.BlockSpec(memory_space=pltpu.VMEM)
    return pl.pallas_call(
        functools.partial(_chol_kernel, n=n, b=block),
        out_shape=(jax.ShapeDtypeStruct(panel.shape, f32), jax.ShapeDtypeStruct(panel.shape, f32)),
        in_specs=[vmem, vmem],
        out_specs=(vmem, vmem),
        scratch_shapes=[
            pltpu.VMEM((n, n), f32),
            pltpu.VMEM((n, n), f32),
            pltpu.VMEM((n, n), f32),
            pltpu.VMEM((block, block), f32),
            pltpu.VMEM((block, block), f32),
            pltpu.VMEM((block, block), f32),
            pltpu.VMEM((block, block), f32),
        ],
        cost_estimate=pl.CostEstimate(
            flops=2 * n * n * n + 4 * panel.shape[0] * n * n, bytes_accessed=5 * n * n * 4, transcendentals=n
        ),
    )(a, panel)


def reduce_by_halving(x, axis, count):
    index = lax.axis_index(axis)
    core = index % 2
    halving = [(1, 1), (2, 8)]
    doubling = [(8, 2), (4, 16), (16, 4)]
    size = x.shape[0]

    def partners(pair):
        return [(i, i ^ pair[i % 2]) for i in range(count)]

    def bit_of(pair):
        mask = jnp.where(core == 0, pair[0], pair[1])
        return (index // mask) % 2

    for pair in halving:
        half = size // 2
        bit = bit_of(pair)
        keep = lax.dynamic_slice_in_dim(x, bit * half, half, 0)
        send = lax.dynamic_slice_in_dim(x, (1 - bit) * half, half, 0)
        x = keep + lax.ppermute(send, axis, partners(pair))
        size = half
    for pair in doubling:
        x = x + lax.ppermute(x, axis, partners(pair))
    for pair in reversed(halving):
        bit = bit_of(pair)
        other = lax.ppermute(x, axis, partners(pair))
        low = jnp.where(bit == 0, x, other)
        high = jnp.where(bit == 0, other, x)
        x = jnp.concatenate([low, high], axis=0)
    return x


def shards(jacobian):
    row_count, par_width = jacobian.shape
    par_count = lax.axis_size("par")
    smp_count = lax.axis_size("smp")
    sample_total = row_count * smp_count
    param_total = par_width * par_count
    col_width = sample_total // par_count
    panel_piece = PANEL // par_count
    row_index = lax.axis_index("smp")
    col_index = lax.axis_index("par")
    f32 = jnp.float32

    gathered = lax.all_gather(jacobian, "smp", axis=0, tiled=True)
    widened = gathered.astype(f32)
    col_mean = jnp.sum(widened, axis=0) / sample_total
    centered = (widened - col_mean).astype(jnp.bfloat16)
    mine = lax.dynamic_slice_in_dim(centered, row_index * row_count, row_count, 0)
    head = centered[:PANEL]
    contract = (((1,), (1,)), ((), ()))

    main_t = lax.dot_general(mine, head, contract, preferred_element_type=f32)
    square = lax.dot_general(head, head, contract, preferred_element_type=f32)
    sq = centered.astype(f32)
    sumsq = jnp.sum(sq * sq)

    block = 128
    per_group = PANEL // block
    pieces = [square[i * block : (i + 1) * block, j * block : (j + 1) * block] for i, j in lower_blocks(per_group)]
    first_pad = len(pieces)
    groups = -(-first_pad // per_group)
    corner = (jnp.arange(block)[:, None] == 0) & (jnp.arange(block)[None, :] == 0)
    pieces.append(jnp.where(corner, sumsq, 0.0))
    while len(pieces) < groups * per_group:
        pieces.append(jnp.zeros((block, block), f32))
    packed = jnp.concatenate(
        [jnp.concatenate(pieces[g * per_group : (g + 1) * per_group], axis=1) for g in range(groups)], axis=0
    )
    panel_in = jnp.concatenate([main_t, packed], axis=0)
    shared = reduce_by_halving(panel_in, "par", par_count) / param_total

    lhs = jnp.concatenate([mine, head], axis=0)
    big = lax.dot_general(lhs, centered, contract, preferred_element_type=f32)
    big = lax.psum_scatter(big, "par", scatter_dimension=1, tiled=True) / param_total
    tile = big[:row_count]
    band_t = big[row_count:]

    panel_g = shared[:row_count]
    square_g = shared[row_count:]
    pad_g, pad_c = divmod(first_pad, per_group)
    trace_total = shared[row_count + pad_g * block, pad_c * block]
    shift_value = shift_scale * trace_total / sample_total

    eye = jnp.arange(PANEL, dtype=jnp.int32)
    global_rows = row_index * row_count + jnp.arange(row_count, dtype=jnp.int32)
    global_cols = col_index * col_width + jnp.arange(col_width, dtype=jnp.int32)
    pr = jnp.arange(groups * block, dtype=jnp.int32)[:, None]
    pc = jnp.arange(PANEL, dtype=jnp.int32)[None, :]
    on_diag = jnp.zeros((groups * block, PANEL), bool)
    for idx, (i, j) in enumerate(lower_blocks(per_group)):
        if i == j:
            g, c = divmod(idx, per_group)
            on_diag = on_diag | ((pr // block == g) & (pc // block == c) & (pr % block == pc % block))
    square_s = square_g + jnp.where(on_diag, shift_value, 0.0)
    panel_s = panel_g + jnp.where(global_rows[:, None] == eye[None, :], shift_value, 0.0)
    band_s = band_t + jnp.where(eye[:, None] == global_cols[None, :], shift_value, 0.0)
    tile_s = tile + jnp.where(global_rows[:, None] == global_cols[None, :], shift_value, 0.0)

    panel_out, projected = chol_and_inverse(square_s, panel_s)
    schur_tile = tile_s - jnp.dot(projected, band_s, precision=HI, preferred_element_type=f32)
    return (panel_out, schur_tile)


def solution(mesh):
    placed = (P("smp", "par"),)
    return jax.shard_map(
        shards,
        mesh=mesh,
        in_specs=placed,
        out_specs=(P("smp", None), P("smp", "par")),
        check_vma=False,
    )
```

```python
import functools

import jax
import jax.numpy as jnp
from jax import lax
from jax.experimental import pallas as pl
from jax.experimental.pallas import tpu as pltpu
from jax.sharding import PartitionSpec as P

PANEL = 512


shift_scale = 0.01


HI = lax.Precision.HIGHEST
NT = (((1,), (1,)), ((), ()))


def lower_blocks(count):
    return [(i, j) for i in range(count) for j in range(i + 1)]


def _chol_kernel(
    sh_ref, off_ref, po_ref, p2_ref, l_ref, w_ref, s_ref, blk_a, blk_b, blk_lt, blk_w, *, n, b, rows_p, pad, scale, shift
):
    nb = n // b
    f32 = jnp.float32
    lower = lax.broadcasted_iota(jnp.int32, (b, b), 0) >= lax.broadcasted_iota(jnp.int32, (b, b), 1)
    diag = lax.broadcasted_iota(jnp.int32, (b, b), 0) == lax.broadcasted_iota(jnp.int32, (b, b), 1)
    first = lax.broadcasted_iota(jnp.int32, (1, b), 1) == 0
    trace_row = sh_ref[pl.ds(rows_p + pad[0] * b, 1), pl.ds(pad[1] * b, b)] * scale
    trace_total = jnp.sum(jnp.where(first, trace_row, 0.0), axis=1, keepdims=True)
    delta = shift[0] * trace_total / shift[1]
    per_group = n // b
    for idx, (i, j) in enumerate(lower_blocks(n // b)):
        g, c = divmod(idx, per_group)
        blk = sh_ref[pl.ds(rows_p + g * b, b), pl.ds(c * b, b)] * scale
        if i == j:
            blk = blk + jnp.where(diag, delta, 0.0)
            s_ref[pl.ds(i * b, b), pl.ds(i * b, b)] = jnp.where(lower, blk, jnp.transpose(blk))
        else:
            s_ref[pl.ds(i * b, b), pl.ds(j * b, b)] = blk
            s_ref[pl.ds(j * b, b), pl.ds(i * b, b)] = jnp.transpose(blk)
    l_ref[...] = jnp.zeros((n, n), f32)
    w_ref[...] = jnp.zeros((n, n), f32)
    rows = lax.broadcasted_iota(jnp.int32, (b, b), 0)
    cols = lax.broadcasted_iota(jnp.int32, (b, b), 1)
    lane = lax.broadcasted_iota(jnp.int32, (1, b), 1)
    sub = lax.broadcasted_iota(jnp.int32, (b, 1), 0)
    for k in range(nb):
        ks = pl.ds(k * b, b)
        blk_a[...] = s_ref[ks, ks]
        blk_b[...] = jnp.where(rows == cols, 1.0, 0.0).astype(f32)

        def step(j, carry):
            whole = blk_a[...]
            row = blk_a[pl.ds(j, 1), :]
            col = jnp.sum(jnp.where(cols == j, whole, 0.0), axis=1, keepdims=True)
            d = jnp.sum(jnp.where(lane == j, row, 0.0), axis=1, keepdims=True)
            r = lax.rsqrt(d)
            v_row = jnp.where(lane >= j, row * r, 0.0)
            v_col = jnp.where(sub >= j, col * r, 0.0)
            blk_a[...] = whole - v_col * v_row
            x = blk_b[pl.ds(j, 1), :] * r
            blk_b[...] = blk_b[...] - v_col * x
            blk_lt[pl.ds(j, 1), :] = v_row
            blk_w[pl.ds(j, 1), :] = x
            return carry

        lax.fori_loop(0, b, step, 0)
        w_kk = blk_w[...]
        l_ref[ks, ks] = jnp.transpose(blk_lt[...])
        w_ref[ks, ks] = w_kk
        if k < nb - 1:
            rest = pl.ds((k + 1) * b, n - (k + 1) * b)
            below = lax.dot_general(s_ref[rest, ks], w_kk, NT, precision=HI, preferred_element_type=f32)
            l_ref[rest, ks] = below
            s_ref[rest, rest] = s_ref[rest, rest] - lax.dot_general(
                below, below, NT, precision=HI, preferred_element_type=f32
            )
    for i in range(1, nb):
        w_ii = w_ref[pl.ds(i * b, b), pl.ds(i * b, b)]
        for j in range(i):
            acc = jnp.zeros((b, b), f32)
            for m in range(j, i):
                acc = acc + jnp.dot(
                    l_ref[pl.ds(i * b, b), pl.ds(m * b, b)],
                    w_ref[pl.ds(m * b, b), pl.ds(j * b, b)],
                    precision=HI,
                    preferred_element_type=f32,
                )
            w_ref[pl.ds(i * b, b), pl.ds(j * b, b)] = -jnp.dot(
                w_ii, acc, precision=HI, preferred_element_type=f32
            )
    inverse = w_ref[...]
    p_rows = lax.broadcasted_iota(jnp.int32, (rows_p, n), 0).astype(f32) + off_ref[:, 0:1]
    p_cols = lax.broadcasted_iota(jnp.int32, (rows_p, n), 1).astype(f32)
    panel_s = sh_ref[pl.ds(0, rows_p), :] * scale + jnp.where(p_rows == p_cols, delta, 0.0)
    panel_out = lax.dot_general(panel_s, inverse, NT, precision=HI, preferred_element_type=f32)
    po_ref[...] = panel_out
    p2_ref[...] = jnp.dot(panel_out, inverse, precision=HI, preferred_element_type=f32)


def chol_and_inverse(shared, offset, rows_p, pad, scale, shift, block=128):
    n = shared.shape[1]
    panel = jax.ShapeDtypeStruct((rows_p, n), jnp.float32)
    f32 = jnp.float32
    vmem = pl.BlockSpec(memory_space=pltpu.VMEM)
    return pl.pallas_call(
        functools.partial(_chol_kernel, n=n, b=block, rows_p=rows_p, pad=pad, scale=scale, shift=shift),
        out_shape=(jax.ShapeDtypeStruct(panel.shape, f32), jax.ShapeDtypeStruct(panel.shape, f32)),
        in_specs=[vmem, vmem],
        out_specs=(vmem, vmem),
        scratch_shapes=[
            pltpu.VMEM((n, n), f32),
            pltpu.VMEM((n, n), f32),
            pltpu.VMEM((n, n), f32),
            pltpu.VMEM((block, block), f32),
            pltpu.VMEM((block, block), f32),
            pltpu.VMEM((block, block), f32),
            pltpu.VMEM((block, block), f32),
        ],
        cost_estimate=pl.CostEstimate(
            flops=2 * n * n * n + 4 * panel.shape[0] * n * n, bytes_accessed=5 * n * n * 4, transcendentals=n
        ),
    )(shared, offset)


def reduce_by_halving(x, axis, count):
    index = lax.axis_index(axis)
    core = index % 2
    halving = [(1, 1), (2, 8)]
    doubling = [(8, 2), (4, 16), (16, 4)]
    size = x.shape[0]

    def partners(pair):
        return [(i, i ^ pair[i % 2]) for i in range(count)]

    def bit_of(pair):
        mask = jnp.where(core == 0, pair[0], pair[1])
        return (index // mask) % 2

    for pair in halving:
        half = size // 2
        bit = bit_of(pair)
        keep = lax.dynamic_slice_in_dim(x, bit * half, half, 0)
        send = lax.dynamic_slice_in_dim(x, (1 - bit) * half, half, 0)
        x = keep + lax.ppermute(send, axis, partners(pair))
        size = half
    for pair in doubling:
        x = x + lax.ppermute(x, axis, partners(pair))
    for pair in reversed(halving):
        bit = bit_of(pair)
        other = lax.ppermute(x, axis, partners(pair))
        low = jnp.where(bit == 0, x, other)
        high = jnp.where(bit == 0, other, x)
        x = jnp.concatenate([low, high], axis=0)
    return x


def shards(jacobian):
    row_count, par_width = jacobian.shape
    par_count = lax.axis_size("par")
    smp_count = lax.axis_size("smp")
    sample_total = row_count * smp_count
    param_total = par_width * par_count
    col_width = sample_total // par_count
    panel_piece = PANEL // par_count
    row_index = lax.axis_index("smp")
    col_index = lax.axis_index("par")
    f32 = jnp.float32

    gathered = lax.all_gather(jacobian, "smp", axis=0, tiled=True)
    widened = gathered.astype(f32)
    col_mean = jnp.sum(widened, axis=0) / sample_total
    centered = (widened - col_mean).astype(jnp.bfloat16)
    mine = lax.dynamic_slice_in_dim(centered, row_index * row_count, row_count, 0)
    head = centered[:PANEL]
    contract = (((1,), (1,)), ((), ()))

    main_t = lax.dot_general(mine, head, contract, preferred_element_type=f32)
    square = lax.dot_general(head, head, contract, preferred_element_type=f32)
    sq = centered.astype(f32)
    sumsq = jnp.sum(sq * sq)

    block = 128
    per_group = PANEL // block
    pieces = [square[i * block : (i + 1) * block, j * block : (j + 1) * block] for i, j in lower_blocks(per_group)]
    first_pad = len(pieces)
    groups = -(-first_pad // per_group)
    corner = (jnp.arange(block)[:, None] == 0) & (jnp.arange(block)[None, :] == 0)
    pieces.append(jnp.where(corner, sumsq, 0.0))
    while len(pieces) < groups * per_group:
        pieces.append(jnp.zeros((block, block), f32))
    packed = jnp.concatenate(
        [jnp.concatenate(pieces[g * per_group : (g + 1) * per_group], axis=1) for g in range(groups)], axis=0
    )
    panel_in = jnp.concatenate([main_t, packed], axis=0)
    shared = reduce_by_halving(panel_in, "par", par_count)

    lhs = jnp.concatenate([mine, head], axis=0)
    big = lax.dot_general(lhs, centered, contract, preferred_element_type=f32)
    big = lax.psum_scatter(big, "par", scatter_dimension=1, tiled=True) / param_total
    tile = big[:row_count]
    band_t = big[row_count:]

    pad_g, pad_c = divmod(first_pad, per_group)
    trace_total = shared[row_count + pad_g * block, pad_c * block] / param_total
    shift_value = shift_scale * trace_total / sample_total

    eye = jnp.arange(PANEL, dtype=jnp.int32)
    global_rows = row_index * row_count + jnp.arange(row_count, dtype=jnp.int32)
    global_cols = col_index * col_width + jnp.arange(col_width, dtype=jnp.int32)
    band_s = band_t + jnp.where(eye[:, None] == global_cols[None, :], shift_value, 0.0)
    tile_s = tile + jnp.where(global_rows[:, None] == global_cols[None, :], shift_value, 0.0)
    offset = jnp.full((1, 128), row_index * row_count, f32)

    panel_out, projected = chol_and_inverse(
        shared, offset, row_count, (pad_g, pad_c), 1.0 / param_total, (shift_scale, float(sample_total))
    )
    schur_tile = tile_s - jnp.dot(projected, band_s, precision=HI, preferred_element_type=f32)
    return (panel_out, schur_tile)


def solution(mesh):
    placed = (P("smp", "par"),)
    return jax.shard_map(
        shards,
        mesh=mesh,
        in_specs=placed,
        out_specs=(P("smp", None), P("smp", "par")),
        check_vma=False,
    )
```

```python
import functools

import jax
import jax.numpy as jnp
from jax import lax
from jax.experimental import pallas as pl
from jax.experimental.pallas import tpu as pltpu
from jax.sharding import PartitionSpec as P

PANEL = 512


shift_scale = 0.01


HI = lax.Precision.HIGHEST
NT = (((1,), (1,)), ((), ()))


def lower_blocks(count):
    return [(i, j) for i in range(count) for j in range(i + 1)]


def _chol_kernel(
    sh_ref, off_ref, po_ref, p2_ref, l_ref, w_ref, s_ref, blk_a, blk_b, blk_lt, blk_w, *, n, b, rows_p, pad, scale, shift
):
    nb = n // b
    f32 = jnp.float32
    lower = lax.broadcasted_iota(jnp.int32, (b, b), 0) >= lax.broadcasted_iota(jnp.int32, (b, b), 1)
    diag = lax.broadcasted_iota(jnp.int32, (b, b), 0) == lax.broadcasted_iota(jnp.int32, (b, b), 1)
    first = lax.broadcasted_iota(jnp.int32, (1, b), 1) == 0
    trace_row = sh_ref[pl.ds(rows_p + pad[0] * b, 1), pl.ds(pad[1] * b, b)] * scale
    trace_total = jnp.sum(jnp.where(first, trace_row, 0.0), axis=1, keepdims=True)
    delta = shift[0] * trace_total / shift[1]
    per_group = n // b
    for idx, (i, j) in enumerate(lower_blocks(n // b)):
        g, c = divmod(idx, per_group)
        blk = sh_ref[pl.ds(rows_p + g * b, b), pl.ds(c * b, b)] * scale
        if i == j:
            blk = blk + jnp.where(diag, delta, 0.0)
            s_ref[pl.ds(i * b, b), pl.ds(i * b, b)] = jnp.where(lower, blk, jnp.transpose(blk))
        else:
            s_ref[pl.ds(i * b, b), pl.ds(j * b, b)] = blk
            s_ref[pl.ds(j * b, b), pl.ds(i * b, b)] = jnp.transpose(blk)
    l_ref[...] = jnp.zeros((n, n), f32)
    w_ref[...] = jnp.zeros((n, n), f32)
    rows = lax.broadcasted_iota(jnp.int32, (b, b), 0)
    cols = lax.broadcasted_iota(jnp.int32, (b, b), 1)
    lane = lax.broadcasted_iota(jnp.int32, (1, b), 1)
    sub = lax.broadcasted_iota(jnp.int32, (b, 1), 0)
    for k in range(nb):
        ks = pl.ds(k * b, b)
        blk_a[...] = s_ref[ks, ks]
        blk_b[...] = jnp.where(rows == cols, 1.0, 0.0).astype(f32)

        def step(j, carry):
            whole = blk_a[...]
            row = blk_a[pl.ds(j, 1), :]
            col = jnp.sum(jnp.where(cols == j, whole, 0.0), axis=1, keepdims=True)
            d = jnp.sum(jnp.where(lane == j, row, 0.0), axis=1, keepdims=True)
            r = lax.rsqrt(d)
            v_row = jnp.where(lane >= j, row * r, 0.0)
            v_col = jnp.where(sub >= j, col * r, 0.0)
            blk_a[...] = whole - v_col * v_row
            x = blk_b[pl.ds(j, 1), :] * r
            blk_b[...] = blk_b[...] - v_col * x
            blk_lt[pl.ds(j, 1), :] = v_row
            blk_w[pl.ds(j, 1), :] = x
            return carry

        lax.fori_loop(0, b, step, 0)
        w_kk = blk_w[...]
        l_ref[ks, ks] = jnp.transpose(blk_lt[...])
        w_ref[ks, ks] = w_kk
        if k < nb - 1:
            rest = pl.ds((k + 1) * b, n - (k + 1) * b)
            below = lax.dot_general(s_ref[rest, ks], w_kk, NT, precision=HI, preferred_element_type=f32)
            l_ref[rest, ks] = below
            s_ref[rest, rest] = s_ref[rest, rest] - lax.dot_general(
                below, below, NT, precision=HI, preferred_element_type=f32
            )
    for i in range(1, nb):
        w_ii = w_ref[pl.ds(i * b, b), pl.ds(i * b, b)]
        for j in range(i):
            acc = jnp.zeros((b, b), f32)
            for m in range(j, i):
                acc = acc + jnp.dot(
                    l_ref[pl.ds(i * b, b), pl.ds(m * b, b)],
                    w_ref[pl.ds(m * b, b), pl.ds(j * b, b)],
                    precision=HI,
                    preferred_element_type=f32,
                )
            w_ref[pl.ds(i * b, b), pl.ds(j * b, b)] = -jnp.dot(
                w_ii, acc, precision=HI, preferred_element_type=f32
            )
    inverse = w_ref[...]
    p_rows = lax.broadcasted_iota(jnp.int32, (rows_p, n), 0).astype(f32) + off_ref[:, 0:1]
    p_cols = lax.broadcasted_iota(jnp.int32, (rows_p, n), 1).astype(f32)
    panel_s = sh_ref[pl.ds(0, rows_p), :] * scale + jnp.where(p_rows == p_cols, delta, 0.0)
    panel_out = lax.dot_general(panel_s, inverse, NT, precision=HI, preferred_element_type=f32)
    po_ref[...] = panel_out
    p2_ref[...] = jnp.dot(panel_out, inverse, precision=HI, preferred_element_type=f32)


def chol_and_inverse(shared, offset, rows_p, pad, scale, shift, block=128):
    n = shared.shape[1]
    panel = jax.ShapeDtypeStruct((rows_p, n), jnp.float32)
    f32 = jnp.float32
    vmem = pl.BlockSpec(memory_space=pltpu.VMEM)
    return pl.pallas_call(
        functools.partial(_chol_kernel, n=n, b=block, rows_p=rows_p, pad=pad, scale=scale, shift=shift),
        out_shape=(jax.ShapeDtypeStruct(panel.shape, f32), jax.ShapeDtypeStruct(panel.shape, f32)),
        in_specs=[vmem, vmem],
        out_specs=(vmem, vmem),
        scratch_shapes=[
            pltpu.VMEM((n, n), f32),
            pltpu.VMEM((n, n), f32),
            pltpu.VMEM((n, n), f32),
            pltpu.VMEM((block, block), f32),
            pltpu.VMEM((block, block), f32),
            pltpu.VMEM((block, block), f32),
            pltpu.VMEM((block, block), f32),
        ],
        cost_estimate=pl.CostEstimate(
            flops=2 * n * n * n + 4 * panel.shape[0] * n * n, bytes_accessed=5 * n * n * 4, transcendentals=n
        ),
    )(shared, offset)


def reduce_by_halving(x, axis, count):
    index = lax.axis_index(axis)
    core = index % 2
    halving = [(1, 1), (2, 8)]
    doubling = [(8, 2), (4, 16), (16, 4)]
    size = x.shape[0]

    def partners(pair):
        return [(i, i ^ pair[i % 2]) for i in range(count)]

    def bit_of(pair):
        mask = jnp.where(core == 0, pair[0], pair[1])
        return (index // mask) % 2

    for pair in halving:
        half = size // 2
        bit = bit_of(pair)
        keep = lax.dynamic_slice_in_dim(x, bit * half, half, 0)
        send = lax.dynamic_slice_in_dim(x, (1 - bit) * half, half, 0)
        x = keep + lax.ppermute(send, axis, partners(pair))
        size = half
    for pair in doubling:
        x = x + lax.ppermute(x, axis, partners(pair))
    for pair in reversed(halving):
        bit = bit_of(pair)
        other = lax.ppermute(x, axis, partners(pair))
        low = jnp.where(bit == 0, x, other)
        high = jnp.where(bit == 0, other, x)
        x = jnp.concatenate([low, high], axis=0)
    return x


def shards(jacobian):
    row_count, par_width = jacobian.shape
    par_count = lax.axis_size("par")
    smp_count = lax.axis_size("smp")
    sample_total = row_count * smp_count
    param_total = par_width * par_count
    col_width = sample_total // par_count
    panel_piece = PANEL // par_count
    row_index = lax.axis_index("smp")
    col_index = lax.axis_index("par")
    f32 = jnp.float32

    gathered = lax.all_gather(jacobian, "smp", axis=0, tiled=True)
    widened = gathered.astype(f32)
    ones = jnp.ones((8, sample_total), jnp.bfloat16)
    col_mean = jnp.dot(ones, gathered, preferred_element_type=f32)[0] / sample_total
    centered = (widened - col_mean).astype(jnp.bfloat16)
    mine = lax.dynamic_slice_in_dim(centered, row_index * row_count, row_count, 0)
    head = centered[:PANEL]
    contract = (((1,), (1,)), ((), ()))

    main_t = lax.dot_general(mine, head, contract, preferred_element_type=f32)
    square = lax.dot_general(head, head, contract, preferred_element_type=f32)
    sq = centered.astype(f32)
    sumsq = jnp.sum(sq * sq)

    block = 128
    per_group = PANEL // block
    pieces = [square[i * block : (i + 1) * block, j * block : (j + 1) * block] for i, j in lower_blocks(per_group)]
    first_pad = len(pieces)
    groups = -(-first_pad // per_group)
    corner = (jnp.arange(block)[:, None] == 0) & (jnp.arange(block)[None, :] == 0)
    pieces.append(jnp.where(corner, sumsq, 0.0))
    while len(pieces) < groups * per_group:
        pieces.append(jnp.zeros((block, block), f32))
    packed = jnp.concatenate(
        [jnp.concatenate(pieces[g * per_group : (g + 1) * per_group], axis=1) for g in range(groups)], axis=0
    )
    panel_in = jnp.concatenate([main_t, packed], axis=0)
    shared = reduce_by_halving(panel_in, "par", par_count)

    lhs = jnp.concatenate([mine, head], axis=0)
    big = lax.dot_general(lhs, centered, contract, preferred_element_type=f32)
    big = lax.psum_scatter(big, "par", scatter_dimension=1, tiled=True) / param_total
    tile = big[:row_count]
    band_t = big[row_count:]

    pad_g, pad_c = divmod(first_pad, per_group)
    trace_total = shared[row_count + pad_g * block, pad_c * block] / param_total
    shift_value = shift_scale * trace_total / sample_total

    eye = jnp.arange(PANEL, dtype=jnp.int32)
    global_rows = row_index * row_count + jnp.arange(row_count, dtype=jnp.int32)
    global_cols = col_index * col_width + jnp.arange(col_width, dtype=jnp.int32)
    band_s = band_t + jnp.where(eye[:, None] == global_cols[None, :], shift_value, 0.0)
    tile_s = tile + jnp.where(global_rows[:, None] == global_cols[None, :], shift_value, 0.0)
    offset = jnp.full((1, 128), row_index * row_count, f32)

    panel_out, projected = chol_and_inverse(
        shared, offset, row_count, (pad_g, pad_c), 1.0 / param_total, (shift_scale, float(sample_total))
    )
    schur_tile = tile_s - jnp.dot(projected, band_s, precision=HI, preferred_element_type=f32)
    return (panel_out, schur_tile)


def solution(mesh):
    placed = (P("smp", "par"),)
    return jax.shard_map(
        shards,
        mesh=mesh,
        in_specs=placed,
        out_specs=(P("smp", None), P("smp", "par")),
        check_vma=False,
    )
```
